32 devices in a mesh: groups: 2 (over y), seq: 4 (over z), tensor: 2 (over x), dp: 2 (over core).
Axes of the slice: x: 2, y: 2, z: 4, core: 2. Of those that a mesh axis runs over, the one named last changes fastest.
Arguments:
- tokens: bfloat16 [4, 1024, 4096], P(('groups', 'dp'), 'seq', 'tensor'), parts along dimension 0, may hold values from -6 to 6
- doc_lengths: int32 [4, 8], P(('groups', 'dp')), parts along dimension 0, may hold values from 1 to 768, 1024 in all within a row
- low_taps: float32 [2, 4096], P(None, 'tensor'), may hold values from 0.66 to 0.75
- high_taps: float32 [2, 4096], P(None, 'tensor'), may hold values from -2.5 to 2.5
- level_weights: float32 [13, 4096], P(None, 'tensor'), may hold values from -2.5 to 2.5
- mix_weight: bfloat16 [4096, 4096], P(None, 'tensor'), may hold values from -0.09375 to 0.09375
- out_grad: bfloat16 [4, 1024, 4096], P(('groups', 'dp'), 'seq', 'tensor'), parts along dimension 0, may hold values from -6 to 6
Outputs:
- result: bfloat16 [4, 1024, 4096], P(('groups', 'dp'), 'seq', 'tensor'), parts along dimension 0
- token_grad: bfloat16 [4, 1024, 4096], P(('groups', 'dp'), 'seq', 'tensor'), parts along dimension 0
- weight_grad: bfloat16 [8192, 4096], P(('groups', 'seq', 'dp'), 'tensor'), parts along dimension 0
- low_grad: float32 [4, 4096], P('groups', 'tensor'), parts along dimension 0
- high_grad: float32 [4, 4096], P('groups', 'tensor'), parts along dimension 0
- level_grad: float32 [26, 4096], P('groups', 'tensor'), parts along dimension 0
The draws below stay inside these ranges and needn't reach their ends.
There are 2 independent parts, one for each index of `groups`. The reference program is written for one: setup_inputs(seed, part) draws one part's arguments, and reference() takes and returns one part's arrays. A program takes and returns all parts, laid end to end along the dimension named above; an argument that names none is the same for every part. Nothing has to cross between parts.
Inputs may be any that keep to these rules, and one draw needn't show every extreme that they name: `doc_lengths`: each row of 8 lengths sums to 1024, and its longest document has exactly 768 positions.
All inputs are finite; a program needn't handle non-finite values.
Results may differ from the reference program's by a relative error of at most 0.015.
Values may be sent and summed in bfloat16 or wider, within the bound.
No kernel may reach another device: no remote copies, remote signals or barrier semaphores. Data moves between devices by JAX's collectives and lax.ppermute only.
A program may use at most 128 MiB of HBM per device.

```python
import math
import jax
import jax.numpy as jnp
import numpy as np
from jax import lax

D = 4096
LEVELS = 12
DOCS = 8
BATCH = 2
LENGTH = 1024
TOKENS = 2048
N_TENSOR = 2


def raised(array, stream_key, source, target, blocks, factor):
    owner, partner = [(jnp.arange(array.shape[dim]) // (array.shape[dim] // blocks)).reshape([-1 if axis == dim else 1 for axis in range(array.ndim)]) for dim in (source, target)]
    chosen = jax.random.permutation(stream_key, blocks)[partner]
    strong = (owner == chosen) | (owner == (partner + blocks // 2) % blocks)
    return jnp.where(strong, factor * array, array)


def block_levels(rng, dims, cuts, low, high):
    gain, own = 1.0, jax.random.fold_in(rng, 6)
    for dim, shards_of in cuts:
        steps = jnp.exp(jax.random.uniform(jax.random.fold_in(own, dim), (shards_of,), jnp.float32, low / len(cuts), high / len(cuts)))
        gain = gain * jnp.repeat(steps, dims[dim] // shards_of).reshape([-1 if axis == dim else 1 for axis in range(len(dims))])
    return gain


def length_profile(count, total, reach, lean):
    portions = [(1 << 20) // math.isqrt(grade ** lean) + 1 for grade in range(2, count + 1)]
    rest, counts = total - reach - (count - 1), [1] * (count - 1)
    while rest > 0:
        free = [i for i in range(count - 1) if counts[i] < reach]
        whole, remaining = sum([portions[i] for i in free]), rest
        for i in free:
            extra = min(reach - counts[i], max(1, remaining * portions[i] // whole), rest)
            counts[i] = counts[i] + extra
            rest = rest - extra
    return np.array([reach] + counts)


def uneven(rng, amount, total, reach, lean):
    if amount == 2:
        one = jax.random.randint(rng, (), max(1, total - reach), min(reach, total - 1) + 1)
        return jnp.stack([one, total - one])
    lengths = jnp.asarray(length_profile(amount, total, reach, lean), jnp.int32)
    twos = (amount - 1) // 2
    source_of, sink = lengths[1:1 + 2 * twos:2], lengths[2:2 + 2 * twos:2]
    slack = jnp.minimum(source_of - 1, reach - sink)
    passed = jax.random.randint(jax.random.fold_in(rng, 1), (twos,), 0, 1 << 20) % (slack + 1)
    lengths = lengths.at[1:1 + 2 * twos:2].set(source_of - passed).at[2:2 + 2 * twos:2].set(sink + passed)
    return lengths[jax.random.permutation(jax.random.fold_in(rng, 2), amount)]


def gaussian(own_key, extent, scale, reach, pieces=(), held_as=jnp.bfloat16):
    values = scale * jax.random.normal(own_key, extent, jnp.float32)
    if pieces:
        values = values * block_levels(own_key, extent, pieces, -0.22, 0.18)
    return jnp.clip(values, -reach, reach).astype(held_as)


def noise_with(key, dims, deviation, most, pieces, heavy, kind=jnp.bfloat16):
    drawn = deviation * jax.random.normal(key, dims, jnp.float32)
    if pieces:
        drawn = drawn * block_levels(key, dims, pieces, -0.22, 0.18)
    return jnp.clip(raised(drawn, jax.random.fold_in(key, 3), *heavy), -most, most).astype(kind)


def setup_inputs(seed: int = 0, part: int = 0) -> dict:
    key_of = jax.random.split(jax.random.key(seed), 8)
    part_keys = jax.random.split(jax.random.fold_in(key_of[7], part), 8)
    return {
        "tokens": gaussian(part_keys[0], (BATCH, LENGTH, D), 1.0, 6.0, ((0, 2), (1, 4), (2, 2))),
        "doc_lengths": jax.vmap(lambda own: uneven(own, DOCS, LENGTH, LENGTH * 3 // 4, 2))(jax.random.split(part_keys[1], BATCH)).reshape((BATCH, DOCS)).astype(jnp.int32),
        "low_taps": jnp.clip(0.66 + 0.089999974 * jax.random.uniform(key_of[2], (2, D), jnp.float32) ** block_levels(key_of[2], (2, D), ((1, 2),), -0.2, 0.2), 0.66, 0.75),
        "high_taps": gaussian(key_of[3], (2, D), 0.7, 2.5, ((1, 2),), jnp.float32),
        "level_weights": gaussian(key_of[4], (LEVELS + 1, D), 0.3, 2.5, ((1, 2),), jnp.float32),
        "mix_weight": gaussian(key_of[5], (D, D), D ** -0.5, 0.09375, ((1, 2),)),
        "out_grad": noise_with(part_keys[6], (BATCH, LENGTH, D), 1.0, 6.0, ((0, 2), (1, 4), (2, 2)), (1, 2, 4, 2.0)),
    }


GELU_SCALE = 0.7978845608028654
GELU_CUBIC = 0.044715


def gelu_value(values):
    tangent = jnp.tanh(GELU_SCALE * (values + GELU_CUBIC * values * values * values))
    return 0.5 * values * (1.0 + tangent)


def gelu_slope(values):
    tangent = jnp.tanh(GELU_SCALE * (values + GELU_CUBIC * values * values * values))
    return 0.5 * (1.0 + tangent) + 0.5 * values * (1.0 - tangent * tangent) * GELU_SCALE * (1.0 + 3.0 * GELU_CUBIC * values * values)


def doc_starts(positions, doc_lengths):
    bounds = jnp.cumsum(doc_lengths, axis=1) - doc_lengths
    before = bounds[:, None, :] <= positions[None, :, None]
    return jnp.max(jnp.where(before, bounds[:, None, :], -1), axis=2)


def tap_mask(positions, starts, spacing):
    return (positions[None, :] - spacing >= starts)[:, :, None]


def shift_down(values, spacing):
    length = values.shape[1]
    if spacing >= length:
        return jnp.zeros_like(values)
    padding = jnp.zeros((values.shape[0], spacing, values.shape[2]), values.dtype)
    return jnp.concatenate([padding, values[:, :length - spacing, :]], axis=1)


def shift_up(values, spacing):
    length = values.shape[1]
    if spacing >= length:
        return jnp.zeros_like(values)
    padding = jnp.zeros((values.shape[0], spacing, values.shape[2]), values.dtype)
    return jnp.concatenate([values[:, spacing:, :], padding], axis=1)


def forward_levels(block, low, high, weights, starts, positions):
    current = block
    summed = jnp.zeros(block.shape, jnp.float32)
    states = [current]
    previous_list = []
    for level_index in range(LEVELS):
        spacing = 2 ** level_index
        shifted = shift_down(current, spacing)
        previous = jnp.where(tap_mask(positions, starts, spacing), shifted, jnp.zeros_like(shifted))
        summed = summed + weights[level_index] * (high[0] * previous + high[1] * current)
        current = (low[0] * previous + low[1] * current).astype(jnp.bfloat16)
        previous_list.append(previous)
        states.append(current)
    summed = summed + weights[LEVELS] * current
    return summed, states, previous_list


def backward_levels(block, summed_grad, low, high, weights, starts, positions):
    recomputed = forward_levels(block, low, high, weights, starts, positions)
    states = recomputed[1]
    previous_list = recomputed[2]
    width = block.shape[2]
    carry_grad = (weights[LEVELS] * summed_grad).astype(jnp.bfloat16)
    weight_sums = [None] * (LEVELS + 1)
    weight_sums[LEVELS] = jnp.sum(summed_grad * states[LEVELS].astype(jnp.float32), axis=(0, 1))
    low_first = jnp.zeros((width,), jnp.float32)
    low_second = jnp.zeros((width,), jnp.float32)
    high_first = jnp.zeros((width,), jnp.float32)
    high_second = jnp.zeros((width,), jnp.float32)
    for level_index in range(LEVELS - 1, -1, -1):
        spacing = 2 ** level_index
        current = states[level_index]
        previous = previous_list[level_index]
        weighted = weights[level_index] * summed_grad
        highpass = high[0] * previous + high[1] * current
        weight_sums[level_index] = jnp.sum(summed_grad * highpass, axis=(0, 1))
        grad_wide = carry_grad.astype(jnp.float32)
        low_first = low_first + jnp.sum(grad_wide * previous.astype(jnp.float32), axis=(0, 1))
        low_second = low_second + jnp.sum(grad_wide * current.astype(jnp.float32), axis=(0, 1))
        high_first = high_first + jnp.sum(weighted * previous.astype(jnp.float32), axis=(0, 1))
        high_second = high_second + jnp.sum(weighted * current.astype(jnp.float32), axis=(0, 1))
        carried = low[0] * carry_grad + high[0] * weighted
        stayed = low[1] * carry_grad + high[1] * weighted
        outgoing = jnp.where(tap_mask(positions, starts, spacing), carried, jnp.zeros_like(carried)).astype(jnp.bfloat16)
        carry_grad = (stayed + shift_up(outgoing, spacing)).astype(jnp.bfloat16)
    taps = jnp.stack([low_first, low_second, high_first, high_second])
    return carry_grad, taps, jnp.stack(weight_sums)


def reference(tokens, doc_lengths, low_taps, high_taps, level_weights, mix_weight, out_grad):
    positions = jnp.arange(LENGTH, dtype=jnp.int32)
    starts = doc_starts(positions, doc_lengths)
    width = min(D, 512)
    blocks = D // width
    grad_scale = float(TOKENS) ** -0.5

    def split_channels(values):
        return values.reshape(values.shape[0], values.shape[1], blocks, width).transpose(2, 0, 1, 3)

    def split_params(values):
        return values.reshape(values.shape[0], blocks, width).transpose(1, 0, 2)

    def join_channels(values):
        return values.transpose(1, 2, 0, 3).reshape(values.shape[1], values.shape[2], D)

    lows = split_params(low_taps)
    highs = split_params(high_taps)
    weights = split_params(level_weights)

    def forward_block(items):
        return forward_levels(items[0], items[1], items[2], items[3], starts, positions)[0]

    summed = join_channels(lax.map(forward_block, (split_channels(tokens), lows, highs, weights)))
    activated = gelu_value(summed).astype(jnp.bfloat16)
    flat_act = activated.reshape(TOKENS, D)
    group_width = D // N_TENSOR
    mixed = jnp.zeros((TOKENS, D), jnp.float32)
    for group in range(N_TENSOR):
        partial_sum = jnp.dot(flat_act[:, group * group_width:(group + 1) * group_width], mix_weight[:, group * group_width:(group + 1) * group_width].T, preferred_element_type=jnp.float32)
        mixed = mixed + lax.optimization_barrier(partial_sum.astype(jnp.bfloat16)).astype(jnp.float32)
    result = (tokens.astype(jnp.float32) + mixed.reshape(BATCH, LENGTH, D)).astype(jnp.bfloat16)
    flat_grad = out_grad.reshape(TOKENS, D)
    act_grad = jnp.dot(flat_grad, mix_weight, preferred_element_type=jnp.float32)
    weight_grad = (jnp.dot(flat_grad.T, flat_act, preferred_element_type=jnp.float32) * grad_scale).astype(jnp.bfloat16)
    summed_grad = act_grad.reshape(BATCH, LENGTH, D) * gelu_slope(summed)

    def backward_block(items):
        return backward_levels(items[0], items[1], items[2], items[3], items[4], starts, positions)

    back_blocks, tap_blocks, level_blocks = lax.map(backward_block, (split_channels(tokens), split_channels(summed_grad), lows, highs, weights))
    token_grad = (out_grad.astype(jnp.float32) + join_channels(back_blocks).astype(jnp.float32)).astype(jnp.bfloat16)
    taps = tap_blocks.transpose(1, 0, 2).reshape(4, D) * grad_scale
    level_grad = level_blocks.transpose(1, 0, 2).reshape(LEVELS + 1, D) * grad_scale
    return result, token_grad, weight_grad, taps[0:2], taps[2:4], level_grad
```

```python
import jax
import jax.numpy as jnp
from jax import lax
from jax.sharding import PartitionSpec as P

GELU_SCALE = 0.7978845608028654
GELU_CUBIC = 0.044715


def shifted_2(block, axis, distance):
    devices = range(lax.axis_size(axis))
    route = [(i - distance, i) for i in devices if i - distance in devices]
    return lax.ppermute(block, axis, route)


def exchange_sum(values, axes):
    for axis in axes:
        size = lax.axis_size(axis)
        if size & (size - 1):
            values = lax.psum(values, axis)
            continue
        step = 1
        while step < size:
            route = [(i, i ^ step) for i in range(size)]
            values = values + lax.ppermute(values, axis, route)
            step *= 2
    return values


def gelu_value(values):
    tangent = jnp.tanh(GELU_SCALE * (values + GELU_CUBIC * values * values * values))
    return 0.5 * values * (1.0 + tangent)


def gelu_slope(values):
    tangent = jnp.tanh(GELU_SCALE * (values + GELU_CUBIC * values * values * values))
    return 0.5 * (1.0 + tangent) + 0.5 * values * (1.0 - tangent * tangent) * GELU_SCALE * (
        1.0 + 3.0 * GELU_CUBIC * values * values
    )


def doc_starts(positions, doc_lengths):
    bounds = jnp.cumsum(doc_lengths, axis=1) - doc_lengths
    before = bounds[:, None, :] <= positions[None, :, None]
    return jnp.max(jnp.where(before, bounds[:, None, :], -1), axis=2)


def tap_mask(positions, starts, spacing):
    return (positions[None, :] - spacing >= starts)[:, :, None]


def shards(tokens, doc_lengths, low_taps, high_taps, level_weights, mix_weight, out_grad):
    batch_size, row_count, channels = tokens.shape
    levels = level_weights.shape[0] - 1
    seq_count = lax.axis_size("seq")
    core_count = lax.axis_size("dp")
    grad_scale = float(batch_size * row_count * seq_count * core_count) ** (-0.5)
    offset = lax.axis_index("seq") * row_count
    positions = offset + jnp.arange(row_count, dtype=jnp.int32)
    starts = doc_starts(positions, doc_lengths)
    shallow = min(levels, row_count.bit_length() - 1)
    summed = jnp.zeros(tokens.shape, jnp.float32)
    states = [tokens]
    previous_list = []
    current = tokens
    for level_index in range(shallow):
        spacing = 2**level_index
        border = shifted_2(current[:, row_count - spacing :, :], "seq", 1)
        shifted = jnp.concatenate([border, current[:, : row_count - spacing, :]], axis=1)
        previous = jnp.where(tap_mask(positions, starts, spacing), shifted, jnp.zeros_like(shifted))
        summed = summed + level_weights[level_index] * (
            high_taps[0] * previous + high_taps[1] * current
        )
        current = (low_taps[0] * previous + low_taps[1] * current).astype(jnp.bfloat16)
        previous_list.append(previous)
        states.append(current)
    for level_index in range(shallow, levels):
        spacing = 2**level_index
        device_hops = spacing // row_count
        if device_hops < seq_count:
            shifted = shifted_2(current, "seq", device_hops)
        else:
            shifted = jnp.zeros_like(current)
        previous = jnp.where(tap_mask(positions, starts, spacing), shifted, jnp.zeros_like(shifted))
        summed = summed + level_weights[level_index] * (
            high_taps[0] * previous + high_taps[1] * current
        )
        current = (low_taps[0] * previous + low_taps[1] * current).astype(jnp.bfloat16)
        previous_list.append(previous)
        states.append(current)
    summed = summed + level_weights[levels] * current
    activated = gelu_value(summed).astype(jnp.bfloat16)
    partial_mix = jnp.einsum(
        "brc,oc->bro", activated, mix_weight, preferred_element_type=jnp.float32
    )
    mixed = lax.psum_scatter(
        partial_mix.astype(jnp.bfloat16), "tensor", scatter_dimension=2, tiled=True
    ).astype(jnp.float32)
    result = (tokens.astype(jnp.float32) + mixed).astype(jnp.bfloat16)
    gathered = lax.all_gather(out_grad, "tensor", axis=2, tiled=True)
    act_grad = jnp.einsum("bro,oc->brc", gathered, mix_weight, preferred_element_type=jnp.float32)
    weight_part = (
        jnp.einsum("bro,brc->oc", gathered, activated, preferred_element_type=jnp.float32)
        * grad_scale
    ).astype(jnp.bfloat16)
    weight_part, act_grad = lax.optimization_barrier((weight_part, act_grad))
    weight_grad = lax.psum_scatter(
        weight_part,
        ("seq", "dp"),
        scatter_dimension=0,
        tiled=True,
    )
    summed_grad = act_grad * gelu_slope(summed)
    carry_grad = (level_weights[levels] * summed_grad).astype(jnp.bfloat16)
    weight_sums = [None] * (levels + 1)
    weight_sums[levels] = jnp.sum(summed_grad * states[levels].astype(jnp.float32), axis=(0, 1))
    low_first = jnp.zeros((channels,), jnp.float32)
    low_second = jnp.zeros((channels,), jnp.float32)
    high_first = jnp.zeros((channels,), jnp.float32)
    high_second = jnp.zeros((channels,), jnp.float32)
    for level_index in range(levels - 1, -1, -1):
        spacing = 2**level_index
        current = states[level_index]
        previous = previous_list[level_index]
        weighted = level_weights[level_index] * summed_grad
        highpass = high_taps[0] * previous + high_taps[1] * current
        weight_sums[level_index] = jnp.sum(summed_grad * highpass, axis=(0, 1))
        grad_wide = carry_grad.astype(jnp.float32)
        low_first = low_first + jnp.sum(grad_wide * previous.astype(jnp.float32), axis=(0, 1))
        low_second = low_second + jnp.sum(grad_wide * current.astype(jnp.float32), axis=(0, 1))
        high_first = high_first + jnp.sum(weighted * previous.astype(jnp.float32), axis=(0, 1))
        high_second = high_second + jnp.sum(weighted * current.astype(jnp.float32), axis=(0, 1))
        carried = low_taps[0] * carry_grad + high_taps[0] * weighted
        stayed = low_taps[1] * carry_grad + high_taps[1] * weighted
        outgoing = jnp.where(
            tap_mask(positions, starts, spacing), carried, jnp.zeros_like(carried)
        ).astype(jnp.bfloat16)
        if level_index < shallow:
            border = shifted_2(outgoing[:, :spacing, :], "seq", -1)
            pulled = jnp.concatenate([outgoing[:, spacing:, :], border], axis=1)
        else:
            device_hops = spacing // row_count
            if device_hops < seq_count:
                pulled = shifted_2(outgoing, "seq", -device_hops)
            else:
                pulled = jnp.zeros_like(outgoing)
        carry_grad = (stayed + pulled).astype(jnp.bfloat16)
    token_grad = (out_grad.astype(jnp.float32) + carry_grad.astype(jnp.float32)).astype(
        jnp.bfloat16
    )
    low_grad = jnp.stack([low_first, low_second]) * grad_scale
    high_grad = jnp.stack([high_first, high_second]) * grad_scale
    level_grad = jnp.stack(weight_sums) * grad_scale
    sums = exchange_sum(jnp.concatenate([low_grad, high_grad, level_grad], axis=0), ("dp", "seq"))
    low_grad, high_grad, level_grad = sums[0:2], sums[2:4], sums[4:]
    return (result, token_grad, weight_grad, low_grad, high_grad, level_grad)


def solution(mesh):
    placed = (
        P(("groups", "dp"), "seq", "tensor"),
        P(("groups", "dp"), None),
        P(None, "tensor"),
        P(None, "tensor"),
        P(None, "tensor"),
        P(None, "tensor"),
        P(("groups", "dp"), "seq", "tensor"),
    )
    return jax.shard_map(
        shards,
        mesh=mesh,
        in_specs=placed,
        out_specs=(
            P(("groups", "dp"), "seq", "tensor"),
            P(("groups", "dp"), "seq", "tensor"),
            P(("groups", "seq", "dp"), "tensor"),
            P("groups", "tensor"),
            P("groups", "tensor"),
            P("groups", "tensor"),
        ),
        check_vma=False,
    )
```

```python
import jax
import jax.numpy as jnp
from jax import lax
from jax.sharding import PartitionSpec as P

GELU_SCALE = 0.7978845608028654
GELU_CUBIC = 0.044715


def shifted_2(block, axis, distance):
    devices = range(lax.axis_size(axis))
    route = [(i - distance, i) for i in devices if i - distance in devices]
    return lax.ppermute(block, axis, route)


def exchange_sum(values, axes):
    for axis in axes:
        size = lax.axis_size(axis)
        if size & (size - 1):
            values = lax.psum(values, axis)
            continue
        step = 1
        while step < size:
            route = [(i, i ^ step) for i in range(size)]
            values = values + lax.ppermute(values, axis, route)
            step *= 2
    return values


def gelu_value(values):
    tangent = jnp.tanh(GELU_SCALE * (values + GELU_CUBIC * values * values * values))
    return 0.5 * values * (1.0 + tangent)


def gelu_slope(values):
    tangent = jnp.tanh(GELU_SCALE * (values + GELU_CUBIC * values * values * values))
    return 0.5 * (1.0 + tangent) + 0.5 * values * (1.0 - tangent * tangent) * GELU_SCALE * (
        1.0 + 3.0 * GELU_CUBIC * values * values
    )


def doc_starts(positions, doc_lengths):
    bounds = jnp.cumsum(doc_lengths, axis=1) - doc_lengths
    before = bounds[:, None, :] <= positions[None, :, None]
    return jnp.max(jnp.where(before, bounds[:, None, :], -1), axis=2)


def tap_mask(positions, starts, spacing):
    return (positions[None, :] - spacing >= starts)[:, :, None]


def shards(tokens, doc_lengths, low_taps, high_taps, level_weights, mix_weight, out_grad):
    batch_size, row_count, channels = tokens.shape
    levels = level_weights.shape[0] - 1
    seq_count = lax.axis_size("seq")
    core_count = lax.axis_size("dp")
    grad_scale = float(batch_size * row_count * seq_count * core_count) ** (-0.5)
    offset = lax.axis_index("seq") * row_count
    positions = offset + jnp.arange(row_count, dtype=jnp.int32)
    starts = doc_starts(positions, doc_lengths)
    shallow = min(levels, row_count.bit_length() - 1)
    gathered = lax.all_gather(out_grad, "tensor", axis=2, tiled=True)
    grad_rows = lax.all_to_all(gathered, ("seq", "dp"), 2, 1, tiled=True)
    summed = jnp.zeros(tokens.shape, jnp.float32)
    states = [tokens]
    previous_list = []
    current = tokens
    for level_index in range(shallow):
        spacing = 2**level_index
        border = shifted_2(current[:, row_count - spacing :, :], "seq", 1)
        shifted = jnp.concatenate([border, current[:, : row_count - spacing, :]], axis=1)
        previous = jnp.where(tap_mask(positions, starts, spacing), shifted, jnp.zeros_like(shifted))
        summed = summed + level_weights[level_index] * (
            high_taps[0] * previous + high_taps[1] * current
        )
        current = (low_taps[0] * previous + low_taps[1] * current).astype(jnp.bfloat16)
        previous_list.append(previous)
        states.append(current)
    for level_index in range(shallow, levels):
        if level_index == shallow:
            grad_rows, current = lax.optimization_barrier((grad_rows, current))
        spacing = 2**level_index
        device_hops = spacing // row_count
        if device_hops < seq_count:
            shifted = shifted_2(current, "seq", device_hops)
        else:
            shifted = jnp.zeros_like(current)
        previous = jnp.where(tap_mask(positions, starts, spacing), shifted, jnp.zeros_like(shifted))
        summed = summed + level_weights[level_index] * (
            high_taps[0] * previous + high_taps[1] * current
        )
        current = (low_taps[0] * previous + low_taps[1] * current).astype(jnp.bfloat16)
        previous_list.append(previous)
        states.append(current)
    summed = summed + level_weights[levels] * current
    activated = gelu_value(summed).astype(jnp.bfloat16)
    partial_mix = jnp.einsum(
        "brc,oc->bro", activated, mix_weight, preferred_element_type=jnp.float32
    )
    mixed = lax.psum_scatter(
        partial_mix.astype(jnp.bfloat16), "tensor", scatter_dimension=2, tiled=True
    ).astype(jnp.float32)
    result = (tokens.astype(jnp.float32) + mixed).astype(jnp.bfloat16)
    act_grad = jnp.einsum("bro,oc->brc", gathered, mix_weight, preferred_element_type=jnp.float32)
    act_all = lax.all_gather(activated, ("seq", "dp"), axis=1, tiled=True)
    weight_grad = (
        jnp.einsum("bto,bti->oi", grad_rows, act_all, preferred_element_type=jnp.float32)
        * grad_scale
    ).astype(jnp.bfloat16)
    summed_grad = act_grad * gelu_slope(summed)
    carry_grad = (level_weights[levels] * summed_grad).astype(jnp.bfloat16)
    weight_sums = [None] * (levels + 1)
    weight_sums[levels] = jnp.sum(summed_grad * states[levels].astype(jnp.float32), axis=(0, 1))
    low_first = jnp.zeros((channels,), jnp.float32)
    low_second = jnp.zeros((channels,), jnp.float32)
    high_first = jnp.zeros((channels,), jnp.float32)
    high_second = jnp.zeros((channels,), jnp.float32)
    for level_index in range(levels - 1, -1, -1):
        if level_index == min(3, levels - 1):
            weight_grad, carry_grad = lax.optimization_barrier((weight_grad, carry_grad))
        spacing = 2**level_index
        current = states[level_index]
        previous = previous_list[level_index]
        weighted = level_weights[level_index] * summed_grad
        highpass = high_taps[0] * previous + high_taps[1] * current
        weight_sums[level_index] = jnp.sum(summed_grad * highpass, axis=(0, 1))
        grad_wide = carry_grad.astype(jnp.float32)
        low_first = low_first + jnp.sum(grad_wide * previous.astype(jnp.float32), axis=(0, 1))
        low_second = low_second + jnp.sum(grad_wide * current.astype(jnp.float32), axis=(0, 1))
        high_first = high_first + jnp.sum(weighted * previous.astype(jnp.float32), axis=(0, 1))
        high_second = high_second + jnp.sum(weighted * current.astype(jnp.float32), axis=(0, 1))
        carried = low_taps[0] * carry_grad + high_taps[0] * weighted
        stayed = low_taps[1] * carry_grad + high_taps[1] * weighted
        outgoing = jnp.where(
            tap_mask(positions, starts, spacing), carried, jnp.zeros_like(carried)
        ).astype(jnp.bfloat16)
        if level_index < shallow:
            border = shifted_2(outgoing[:, :spacing, :], "seq", -1)
            pulled = jnp.concatenate([outgoing[:, spacing:, :], border], axis=1)
        else:
            device_hops = spacing // row_count
            if device_hops < seq_count:
                pulled = shifted_2(outgoing, "seq", -device_hops)
            else:
                pulled = jnp.zeros_like(outgoing)
        carry_grad = (stayed + pulled).astype(jnp.bfloat16)
    token_grad = (out_grad.astype(jnp.float32) + carry_grad.astype(jnp.float32)).astype(
        jnp.bfloat16
    )
    low_grad = jnp.stack([low_first, low_second]) * grad_scale
    high_grad = jnp.stack([high_first, high_second]) * grad_scale
    level_grad = jnp.stack(weight_sums) * grad_scale
    sums = exchange_sum(jnp.concatenate([low_grad, high_grad, level_grad], axis=0), ("dp", "seq"))
    low_grad, high_grad, level_grad = sums[0:2], sums[2:4], sums[4:]
    return (result, token_grad, weight_grad, low_grad, high_grad, level_grad)


def solution(mesh):
    placed = (
        P(("groups", "dp"), "seq", "tensor"),
        P(("groups", "dp"), None),
        P(None, "tensor"),
        P(None, "tensor"),
        P(None, "tensor"),
        P(None, "tensor"),
        P(("groups", "dp"), "seq", "tensor"),
    )
    return jax.shard_map(
        shards,
        mesh=mesh,
        in_specs=placed,
        out_specs=(
            P(("groups", "dp"), "seq", "tensor"),
            P(("groups", "dp"), "seq", "tensor"),
            P(("groups", "seq", "dp"), "tensor"),
            P("groups", "tensor"),
            P("groups", "tensor"),
            P("groups", "tensor"),
        ),
        check_vma=False,
    )
```

```python
import jax
import jax.numpy as jnp
from jax import lax
from jax.sharding import PartitionSpec as P

GELU_SCALE = 0.7978845608028654
GELU_CUBIC = 0.044715


def shifted_2(block, axis, distance):
    devices = range(lax.axis_size(axis))
    route = [(i - distance, i) for i in devices if i - distance in devices]
    return lax.ppermute(block, axis, route)


def exchange_sum(values, axes):
    for axis in axes:
        size = lax.axis_size(axis)
        if size & (size - 1):
            values = lax.psum(values, axis)
            continue
        step = 1
        while step < size:
            route = [(i, i ^ step) for i in range(size)]
            values = values + lax.ppermute(values, axis, route)
            step *= 2
    return values


def gelu_value(values):
    tangent = jnp.tanh(GELU_SCALE * (values + GELU_CUBIC * values * values * values))
    return 0.5 * values * (1.0 + tangent)


def gelu_slope(values):
    tangent = jnp.tanh(GELU_SCALE * (values + GELU_CUBIC * values * values * values))
    return 0.5 * (1.0 + tangent) + 0.5 * values * (1.0 - tangent * tangent) * GELU_SCALE * (
        1.0 + 3.0 * GELU_CUBIC * values * values
    )


def doc_starts(positions, doc_lengths):
    bounds = jnp.cumsum(doc_lengths, axis=1) - doc_lengths
    before = bounds[:, None, :] <= positions[None, :, None]
    return jnp.max(jnp.where(before, bounds[:, None, :], -1), axis=2)


def tap_mask(positions, starts, spacing):
    return (positions[None, :] - spacing >= starts)[:, :, None]


def shards(tokens, doc_lengths, low_taps, high_taps, level_weights, mix_weight, out_grad):
    batch_size, row_count, channels = tokens.shape
    levels = level_weights.shape[0] - 1
    seq_count = lax.axis_size("seq")
    core_count = lax.axis_size("dp")
    grad_scale = float(batch_size * row_count * seq_count * core_count) ** (-0.5)
    offset = lax.axis_index("seq") * row_count
    positions = offset + jnp.arange(row_count, dtype=jnp.int32)
    starts = doc_starts(positions, doc_lengths)
    shallow = min(levels, row_count.bit_length() - 1)
    summed = jnp.zeros(tokens.shape, jnp.float32)
    states = [tokens]
    previous_list = []
    current = tokens
    wide_positions = offset - row_count + jnp.arange(2 * row_count, dtype=jnp.int32)
    wide_starts = doc_starts(wide_positions, doc_lengths)
    wide = jnp.concatenate([shifted_2(tokens, "seq", 1), tokens], axis=1)
    for level_index in range(shallow):
        spacing = 2**level_index
        padding = jnp.zeros((wide.shape[0], spacing, wide.shape[2]), wide.dtype)
        shifted = jnp.concatenate([padding, wide[:, : 2 * row_count - spacing, :]], axis=1)
        previous_wide = jnp.where(
            tap_mask(wide_positions, wide_starts, spacing), shifted, jnp.zeros_like(shifted)
        )
        previous = previous_wide[:, row_count:, :]
        summed = summed + level_weights[level_index] * (
            high_taps[0] * previous + high_taps[1] * current
        )
        wide = (low_taps[0] * previous_wide + low_taps[1] * wide).astype(jnp.bfloat16)
        current = wide[:, row_count:, :]
        previous_list.append(previous)
        states.append(current)
    for level_index in range(shallow, levels):
        spacing = 2**level_index
        device_hops = spacing // row_count
        if device_hops < seq_count:
            shifted = shifted_2(current, "seq", device_hops)
        else:
            shifted = jnp.zeros_like(current)
        previous = jnp.where(tap_mask(positions, starts, spacing), shifted, jnp.zeros_like(shifted))
        summed = summed + level_weights[level_index] * (
            high_taps[0] * previous + high_taps[1] * current
        )
        current = (low_taps[0] * previous + low_taps[1] * current).astype(jnp.bfloat16)
        previous_list.append(previous)
        states.append(current)
    summed = summed + level_weights[levels] * current
    activated = gelu_value(summed).astype(jnp.bfloat16)
    partial_mix = jnp.einsum(
        "brc,oc->bro", activated, mix_weight, preferred_element_type=jnp.float32
    )
    mixed = lax.psum_scatter(
        partial_mix.astype(jnp.bfloat16), "tensor", scatter_dimension=2, tiled=True
    ).astype(jnp.float32)
    result = (tokens.astype(jnp.float32) + mixed).astype(jnp.bfloat16)
    gathered = lax.all_gather(out_grad, "tensor", axis=2, tiled=True)
    act_grad = jnp.einsum("bro,oc->brc", gathered, mix_weight, preferred_element_type=jnp.float32)
    weight_part = (
        jnp.einsum("bro,brc->oc", gathered, activated, preferred_element_type=jnp.float32)
        * grad_scale
    ).astype(jnp.bfloat16)
    weight_part, act_grad = lax.optimization_barrier((weight_part, act_grad))
    weight_grad = lax.psum_scatter(
        weight_part,
        ("seq", "dp"),
        scatter_dimension=0,
        tiled=True,
    )
    summed_grad = act_grad * gelu_slope(summed)
    carry_grad = (level_weights[levels] * summed_grad).astype(jnp.bfloat16)
    weight_sums = [None] * (levels + 1)
    weight_sums[levels] = jnp.sum(summed_grad * states[levels].astype(jnp.float32), axis=(0, 1))
    low_first = jnp.zeros((channels,), jnp.float32)
    low_second = jnp.zeros((channels,), jnp.float32)
    high_first = jnp.zeros((channels,), jnp.float32)
    high_second = jnp.zeros((channels,), jnp.float32)
    for level_index in range(levels - 1, -1, -1):
        spacing = 2**level_index
        current = states[level_index]
        previous = previous_list[level_index]
        weighted = level_weights[level_index] * summed_grad
        highpass = high_taps[0] * previous + high_taps[1] * current
        weight_sums[level_index] = jnp.sum(summed_grad * highpass, axis=(0, 1))
        grad_wide = carry_grad.astype(jnp.float32)
        low_first = low_first + jnp.sum(grad_wide * previous.astype(jnp.float32), axis=(0, 1))
        low_second = low_second + jnp.sum(grad_wide * current.astype(jnp.float32), axis=(0, 1))
        high_first = high_first + jnp.sum(weighted * previous.astype(jnp.float32), axis=(0, 1))
        high_second = high_second + jnp.sum(weighted * current.astype(jnp.float32), axis=(0, 1))
        carried = low_taps[0] * carry_grad + high_taps[0] * weighted
        stayed = low_taps[1] * carry_grad + high_taps[1] * weighted
        outgoing = jnp.where(
            tap_mask(positions, starts, spacing), carried, jnp.zeros_like(carried)
        ).astype(jnp.bfloat16)
        if level_index < shallow:
            border = shifted_2(outgoing[:, :spacing, :], "seq", -1)
            pulled = jnp.concatenate([outgoing[:, spacing:, :], border], axis=1)
        else:
            device_hops = spacing // row_count
            if device_hops < seq_count:
                pulled = shifted_2(outgoing, "seq", -device_hops)
            else:
                pulled = jnp.zeros_like(outgoing)
        carry_grad = (stayed + pulled).astype(jnp.bfloat16)
    token_grad = (out_grad.astype(jnp.float32) + carry_grad.astype(jnp.float32)).astype(
        jnp.bfloat16
    )
    low_grad = jnp.stack([low_first, low_second]) * grad_scale
    high_grad = jnp.stack([high_first, high_second]) * grad_scale
    level_grad = jnp.stack(weight_sums) * grad_scale
    sums = exchange_sum(jnp.concatenate([low_grad, high_grad, level_grad], axis=0), ("dp", "seq"))
    low_grad, high_grad, level_grad = sums[0:2], sums[2:4], sums[4:]
    return (result, token_grad, weight_grad, low_grad, high_grad, level_grad)


def solution(mesh):
    placed = (
        P(("groups", "dp"), "seq", "tensor"),
        P(("groups", "dp"), None),
        P(None, "tensor"),
        P(None, "tensor"),
        P(None, "tensor"),
        P(None, "tensor"),
        P(("groups", "dp"), "seq", "tensor"),
    )
    return jax.shard_map(
        shards,
        mesh=mesh,
        in_specs=placed,
        out_specs=(
            P(("groups", "dp"), "seq", "tensor"),
            P(("groups", "dp"), "seq", "tensor"),
            P(("groups", "seq", "dp"), "tensor"),
            P("groups", "tensor"),
            P("groups", "tensor"),
            P("groups", "tensor"),
        ),
        check_vma=False,
    )
```

```python
import jax
import jax.numpy as jnp
from jax import lax
from jax.sharding import PartitionSpec as P

GELU_SCALE = 0.7978845608028654
GELU_CUBIC = 0.044715


def shifted_2(block, axis, distance):
    devices = range(lax.axis_size(axis))
    route = [(i - distance, i) for i in devices if i - distance in devices]
    return lax.ppermute(block, axis, route)


def exchange_sum(values, axes):
    for axis in axes:
        size = lax.axis_size(axis)
        if size & (size - 1):
            values = lax.psum(values, axis)
            continue
        step = 1
        while step < size:
            route = [(i, i ^ step) for i in range(size)]
            values = values + lax.ppermute(values, axis, route)
            step *= 2
    return values


def exchange_scatter(values, axis):
    size = lax.axis_size(axis)
    me = lax.axis_index(axis)
    width = values.shape[-1] // size
    chunks = values.reshape(values.shape[:-1] + (size, width))

    def chunk(index):
        return lax.dynamic_index_in_dim(chunks, index, axis=chunks.ndim - 2, keepdims=False)

    total = chunk(me).astype(jnp.float32)
    for step in range(1, size):
        route = [(i, (i + step) % size) for i in range(size)]
        total = total + lax.ppermute(chunk((me + step) % size), axis, route).astype(jnp.float32)
    return total


def gelu_value(values):
    tangent = jnp.tanh(GELU_SCALE * (values + GELU_CUBIC * values * values * values))
    return 0.5 * values * (1.0 + tangent)


def gelu_slope(values):
    tangent = jnp.tanh(GELU_SCALE * (values + GELU_CUBIC * values * values * values))
    return 0.5 * (1.0 + tangent) + 0.5 * values * (1.0 - tangent * tangent) * GELU_SCALE * (
        1.0 + 3.0 * GELU_CUBIC * values * values
    )


def doc_starts(positions, doc_lengths):
    bounds = jnp.cumsum(doc_lengths, axis=1) - doc_lengths
    before = bounds[:, None, :] <= positions[None, :, None]
    return jnp.max(jnp.where(before, bounds[:, None, :], -1), axis=2)


def tap_mask(positions, starts, spacing):
    return (positions[None, :] - spacing >= starts)[:, :, None]


def shards(tokens, doc_lengths, low_taps, high_taps, level_weights, mix_weight, out_grad):
    batch_size, row_count, channels = tokens.shape
    levels = level_weights.shape[0] - 1
    seq_count = lax.axis_size("seq")
    core_count = lax.axis_size("dp")
    grad_scale = float(batch_size * row_count * seq_count * core_count) ** (-0.5)
    offset = lax.axis_index("seq") * row_count
    positions = offset + jnp.arange(row_count, dtype=jnp.int32)
    starts = doc_starts(positions, doc_lengths)
    shallow = min(levels, row_count.bit_length() - 1)
    summed = jnp.zeros(tokens.shape, jnp.float32)
    states = [tokens]
    previous_list = []
    current = tokens
    wide_positions = offset - row_count + jnp.arange(2 * row_count, dtype=jnp.int32)
    wide_starts = doc_starts(wide_positions, doc_lengths)
    wide = jnp.concatenate([shifted_2(tokens, "seq", 1), tokens], axis=1)
    for level_index in range(shallow):
        spacing = 2**level_index
        padding = jnp.zeros((wide.shape[0], spacing, wide.shape[2]), wide.dtype)
        shifted = jnp.concatenate([padding, wide[:, : 2 * row_count - spacing, :]], axis=1)
        previous_wide = jnp.where(
            tap_mask(wide_positions, wide_starts, spacing), shifted, jnp.zeros_like(shifted)
        )
        previous = previous_wide[:, row_count:, :]
        summed = summed + level_weights[level_index] * (
            high_taps[0] * previous + high_taps[1] * current
        )
        wide = (low_taps[0] * previous_wide + low_taps[1] * wide).astype(jnp.bfloat16)
        current = wide[:, row_count:, :]
        previous_list.append(previous)
        states.append(current)
    for level_index in range(shallow, levels):
        spacing = 2**level_index
        device_hops = spacing // row_count
        if device_hops < seq_count:
            shifted = shifted_2(current, "seq", device_hops)
        else:
            shifted = jnp.zeros_like(current)
        previous = jnp.where(tap_mask(positions, starts, spacing), shifted, jnp.zeros_like(shifted))
        summed = summed + level_weights[level_index] * (
            high_taps[0] * previous + high_taps[1] * current
        )
        current = (low_taps[0] * previous + low_taps[1] * current).astype(jnp.bfloat16)
        previous_list.append(previous)
        states.append(current)
    summed = summed + level_weights[levels] * current
    activated = gelu_value(summed).astype(jnp.bfloat16)
    gathered = lax.all_gather(out_grad, "tensor", axis=2, tiled=True)
    weight_part = (
        jnp.einsum("bro,brc->oc", gathered, activated, preferred_element_type=jnp.float32)
        * grad_scale
    ).astype(jnp.bfloat16)
    weight_part, activated, gathered = lax.optimization_barrier((weight_part, activated, gathered))
    weight_grad = lax.psum_scatter(
        weight_part,
        ("seq", "dp"),
        scatter_dimension=0,
        tiled=True,
    )
    act_grad = jnp.einsum("bro,oc->brc", gathered, mix_weight, preferred_element_type=jnp.float32)
    act_grad, activated = lax.optimization_barrier((act_grad, activated))
    partial_mix = jnp.einsum(
        "brc,oc->bro", activated, mix_weight, preferred_element_type=jnp.float32
    )
    mix_part = partial_mix.astype(jnp.bfloat16)
    summed_grad = act_grad * gelu_slope(summed)
    carry_grad = (level_weights[levels] * summed_grad).astype(jnp.bfloat16)
    weight_sums = [None] * (levels + 1)
    weight_sums[levels] = jnp.sum(summed_grad * states[levels].astype(jnp.float32), axis=(0, 1))
    low_first = jnp.zeros((channels,), jnp.float32)
    low_second = jnp.zeros((channels,), jnp.float32)
    high_first = jnp.zeros((channels,), jnp.float32)
    high_second = jnp.zeros((channels,), jnp.float32)
    for level_index in range(levels - 1, -1, -1):
        spacing = 2**level_index
        current = states[level_index]
        previous = previous_list[level_index]
        weighted = level_weights[level_index] * summed_grad
        highpass = high_taps[0] * previous + high_taps[1] * current
        weight_sums[level_index] = jnp.sum(summed_grad * highpass, axis=(0, 1))
        grad_wide = carry_grad.astype(jnp.float32)
        low_first = low_first + jnp.sum(grad_wide * previous.astype(jnp.float32), axis=(0, 1))
        low_second = low_second + jnp.sum(grad_wide * current.astype(jnp.float32), axis=(0, 1))
        high_first = high_first + jnp.sum(weighted * previous.astype(jnp.float32), axis=(0, 1))
        high_second = high_second + jnp.sum(weighted * current.astype(jnp.float32), axis=(0, 1))
        carried = low_taps[0] * carry_grad + high_taps[0] * weighted
        stayed = low_taps[1] * carry_grad + high_taps[1] * weighted
        outgoing = jnp.where(
            tap_mask(positions, starts, spacing), carried, jnp.zeros_like(carried)
        ).astype(jnp.bfloat16)
        if level_index < shallow:
            border = shifted_2(outgoing[:, :spacing, :], "seq", -1)
            pulled = jnp.concatenate([outgoing[:, spacing:, :], border], axis=1)
        else:
            device_hops = spacing // row_count
            if device_hops < seq_count:
                pulled = shifted_2(outgoing, "seq", -device_hops)
            else:
                pulled = jnp.zeros_like(outgoing)
        carry_grad = (stayed + pulled).astype(jnp.bfloat16)
    mixed = exchange_scatter(mix_part, "tensor")
    result = (tokens.astype(jnp.float32) + mixed).astype(jnp.bfloat16)
    token_grad = (out_grad.astype(jnp.float32) + carry_grad.astype(jnp.float32)).astype(
        jnp.bfloat16
    )
    low_grad = jnp.stack([low_first, low_second]) * grad_scale
    high_grad = jnp.stack([high_first, high_second]) * grad_scale
    level_grad = jnp.stack(weight_sums) * grad_scale
    sums = exchange_sum(jnp.concatenate([low_grad, high_grad, level_grad], axis=0), ("dp", "seq"))
    low_grad, high_grad, level_grad = sums[0:2], sums[2:4], sums[4:]
    return (result, token_grad, weight_grad, low_grad, high_grad, level_grad)


def solution(mesh):
    placed = (
        P(("groups", "dp"), "seq", "tensor"),
        P(("groups", "dp"), None),
        P(None, "tensor"),
        P(None, "tensor"),
        P(None, "tensor"),
        P(None, "tensor"),
        P(("groups", "dp"), "seq", "tensor"),
    )
    return jax.shard_map(
        shards,
        mesh=mesh,
        in_specs=placed,
        out_specs=(
            P(("groups", "dp"), "seq", "tensor"),
            P(("groups", "dp"), "seq", "tensor"),
            P(("groups", "seq", "dp"), "tensor"),
            P("groups", "tensor"),
            P("groups", "tensor"),
            P("groups", "tensor"),
        ),
        check_vma=False,
    )
```

```python
import jax
import jax.numpy as jnp
from jax import lax
from jax.sharding import PartitionSpec as P

GELU_SCALE = 0.7978845608028654
GELU_CUBIC = 0.044715


def shifted_2(block, axis, distance):
    devices = range(lax.axis_size(axis))
    route = [(i - distance, i) for i in devices if i - distance in devices]
    rows = block.shape[1]
    if rows >= 256 and rows % 2 == 0:
        half = rows // 2
        return jnp.concatenate(
            [lax.ppermute(block[:, :half], axis, route), lax.ppermute(block[:, half:], axis, route)],
            axis=1,
        )
    return lax.ppermute(block, axis, route)


def exchange_sum(values, axes):
    for axis in axes:
        size = lax.axis_size(axis)
        if size & (size - 1):
            values = lax.psum(values, axis)
            continue
        step = 1
        while step < size:
            route = [(i, i ^ step) for i in range(size)]
            values = values + lax.ppermute(values, axis, route)
            step *= 2
    return values


def gelu_value(values):
    tangent = jnp.tanh(GELU_SCALE * (values + GELU_CUBIC * values * values * values))
    return 0.5 * values * (1.0 + tangent)


def gelu_slope(values):
    tangent = jnp.tanh(GELU_SCALE * (values + GELU_CUBIC * values * values * values))
    return 0.5 * (1.0 + tangent) + 0.5 * values * (1.0 - tangent * tangent) * GELU_SCALE * (
        1.0 + 3.0 * GELU_CUBIC * values * values
    )


def doc_starts(positions, doc_lengths):
    bounds = jnp.cumsum(doc_lengths, axis=1) - doc_lengths
    before = bounds[:, None, :] <= positions[None, :, None]
    return jnp.max(jnp.where(before, bounds[:, None, :], -1), axis=2)


def tap_mask(positions, starts, spacing):
    return (positions[None, :] - spacing >= starts)[:, :, None]


def shards(tokens, doc_lengths, low_taps, high_taps, level_weights, mix_weight, out_grad):
    batch_size, row_count, channels = tokens.shape
    levels = level_weights.shape[0] - 1
    seq_count = lax.axis_size("seq")
    core_count = lax.axis_size("dp")
    grad_scale = float(batch_size * row_count * seq_count * core_count) ** (-0.5)
    offset = lax.axis_index("seq") * row_count
    positions = offset + jnp.arange(row_count, dtype=jnp.int32)
    starts = doc_starts(positions, doc_lengths)
    shallow = min(levels, row_count.bit_length() - 1)
    summed = jnp.zeros(tokens.shape, jnp.float32)
    states = [tokens]
    previous_list = []
    current = tokens
    wide_positions = offset - row_count + jnp.arange(2 * row_count, dtype=jnp.int32)
    wide_starts = doc_starts(wide_positions, doc_lengths)
    wide = jnp.concatenate([shifted_2(tokens, "seq", 1), tokens], axis=1)
    for level_index in range(shallow):
        spacing = 2**level_index
        padding = jnp.zeros((wide.shape[0], spacing, wide.shape[2]), wide.dtype)
        shifted = jnp.concatenate([padding, wide[:, : 2 * row_count - spacing, :]], axis=1)
        previous_wide = jnp.where(
            tap_mask(wide_positions, wide_starts, spacing), shifted, jnp.zeros_like(shifted)
        )
        previous = previous_wide[:, row_count:, :]
        summed = summed + level_weights[level_index] * (
            high_taps[0] * previous + high_taps[1] * current
        )
        wide = (low_taps[0] * previous_wide + low_taps[1] * wide).astype(jnp.bfloat16)
        current = wide[:, row_count:, :]
        previous_list.append(previous)
        states.append(current)
    for level_index in range(shallow, levels):
        spacing = 2**level_index
        device_hops = spacing // row_count
        if device_hops < seq_count:
            shifted = shifted_2(current, "seq", device_hops)
        else:
            shifted = jnp.zeros_like(current)
        previous = jnp.where(tap_mask(positions, starts, spacing), shifted, jnp.zeros_like(shifted))
        summed = summed + level_weights[level_index] * (
            high_taps[0] * previous + high_taps[1] * current
        )
        current = (low_taps[0] * previous + low_taps[1] * current).astype(jnp.bfloat16)
        previous_list.append(previous)
        states.append(current)
    summed = summed + level_weights[levels] * current
    activated = gelu_value(summed).astype(jnp.bfloat16)
    partial_mix = jnp.einsum(
        "brc,oc->bro", activated, mix_weight, preferred_element_type=jnp.float32
    )
    mixed = lax.psum_scatter(
        partial_mix.astype(jnp.bfloat16), "tensor", scatter_dimension=2, tiled=True
    ).astype(jnp.float32)
    result = (tokens.astype(jnp.float32) + mixed).astype(jnp.bfloat16)
    gathered = lax.all_gather(out_grad, "tensor", axis=2, tiled=True)
    act_grad = jnp.einsum("bro,oc->brc", gathered, mix_weight, preferred_element_type=jnp.float32)
    weight_part = (
        jnp.einsum("bro,brc->oc", gathered, activated, preferred_element_type=jnp.float32)
        * grad_scale
    ).astype(jnp.bfloat16)
    weight_part, act_grad = lax.optimization_barrier((weight_part, act_grad))
    weight_grad = lax.psum_scatter(
        weight_part,
        ("seq", "dp"),
        scatter_dimension=0,
        tiled=True,
    )
    summed_grad = act_grad * gelu_slope(summed)
    carry_grad = (level_weights[levels] * summed_grad).astype(jnp.bfloat16)
    weight_sums = [None] * (levels + 1)
    weight_sums[levels] = jnp.sum(summed_grad * states[levels].astype(jnp.float32), axis=(0, 1))
    low_first = jnp.zeros((channels,), jnp.float32)
    low_second = jnp.zeros((channels,), jnp.float32)
    high_first = jnp.zeros((channels,), jnp.float32)
    high_second = jnp.zeros((channels,), jnp.float32)
    for level_index in range(levels - 1, -1, -1):
        spacing = 2**level_index
        current = states[level_index]
        previous = previous_list[level_index]
        weighted = level_weights[level_index] * summed_grad
        highpass = high_taps[0] * previous + high_taps[1] * current
        weight_sums[level_index] = jnp.sum(summed_grad * highpass, axis=(0, 1))
        grad_wide = carry_grad.astype(jnp.float32)
        low_first = low_first + jnp.sum(grad_wide * previous.astype(jnp.float32), axis=(0, 1))
        low_second = low_second + jnp.sum(grad_wide * current.astype(jnp.float32), axis=(0, 1))
        high_first = high_first + jnp.sum(weighted * previous.astype(jnp.float32), axis=(0, 1))
        high_second = high_second + jnp.sum(weighted * current.astype(jnp.float32), axis=(0, 1))
        carried = low_taps[0] * carry_grad + high_taps[0] * weighted
        stayed = low_taps[1] * carry_grad + high_taps[1] * weighted
        outgoing = jnp.where(
            tap_mask(positions, starts, spacing), carried, jnp.zeros_like(carried)
        ).astype(jnp.bfloat16)
        if level_index < shallow:
            border = shifted_2(outgoing[:, :spacing, :], "seq", -1)
            pulled = jnp.concatenate([outgoing[:, spacing:, :], border], axis=1)
        else:
            device_hops = spacing // row_count
            if device_hops < seq_count:
                pulled = shifted_2(outgoing, "seq", -device_hops)
            else:
                pulled = jnp.zeros_like(outgoing)
        carry_grad = (stayed + pulled).astype(jnp.bfloat16)
    token_grad = (out_grad.astype(jnp.float32) + carry_grad.astype(jnp.float32)).astype(
        jnp.bfloat16
    )
    low_grad = jnp.stack([low_first, low_second]) * grad_scale
    high_grad = jnp.stack([high_first, high_second]) * grad_scale
    level_grad = jnp.stack(weight_sums) * grad_scale
    sums = exchange_sum(jnp.concatenate([low_grad, high_grad, level_grad], axis=0), ("dp", "seq"))
    low_grad, high_grad, level_grad = sums[0:2], sums[2:4], sums[4:]
    return (result, token_grad, weight_grad, low_grad, high_grad, level_grad)


def solution(mesh):
    placed = (
        P(("groups", "dp"), "seq", "tensor"),
        P(("groups", "dp"), None),
        P(None, "tensor"),
        P(None, "tensor"),
        P(None, "tensor"),
        P(None, "tensor"),
        P(("groups", "dp"), "seq", "tensor"),
    )
    return jax.shard_map(
        shards,
        mesh=mesh,
        in_specs=placed,
        out_specs=(
            P(("groups", "dp"), "seq", "tensor"),
            P(("groups", "dp"), "seq", "tensor"),
            P(("groups", "seq", "dp"), "tensor"),
            P("groups", "tensor"),
            P("groups", "tensor"),
            P("groups", "tensor"),
        ),
        check_vma=False,
    )
```

```python
import jax
import jax.numpy as jnp
from jax import lax
from jax.sharding import PartitionSpec as P

GELU_SCALE = 0.7978845608028654
GELU_CUBIC = 0.044715


def shifted_2(block, axis, distance):
    devices = range(lax.axis_size(axis))
    route = [(i - distance, i) for i in devices if i - distance in devices]
    return lax.ppermute(block, axis, route)


def exchange_sum(values, axes):
    for axis in axes:
        size = lax.axis_size(axis)
        if size & (size - 1):
            values = lax.psum(values, axis)
            continue
        step = 1
        while step < size:
            route = [(i, i ^ step) for i in range(size)]
            values = values + lax.ppermute(values, axis, route)
            step *= 2
    return values


def gelu_value(values):
    tangent = jnp.tanh(GELU_SCALE * (values + GELU_CUBIC * values * values * values))
    return 0.5 * values * (1.0 + tangent)


def gelu_slope(values):
    tangent = jnp.tanh(GELU_SCALE * (values + GELU_CUBIC * values * values * values))
    return 0.5 * (1.0 + tangent) + 0.5 * values * (1.0 - tangent * tangent) * GELU_SCALE * (
        1.0 + 3.0 * GELU_CUBIC * values * values
    )


def doc_starts(positions, doc_lengths):
    bounds = jnp.cumsum(doc_lengths, axis=1) - doc_lengths
    before = bounds[:, None, :] <= positions[None, :, None]
    return jnp.max(jnp.where(before, bounds[:, None, :], -1), axis=2)


def tap_mask(positions, starts, spacing):
    return (positions[None, :] - spacing >= starts)[:, :, None]


def shards(tokens, doc_lengths, low_taps, high_taps, level_weights, mix_weight, out_grad):
    batch_size, row_count, channels = tokens.shape
    levels = level_weights.shape[0] - 1
    seq_count = lax.axis_size("seq")
    core_count = lax.axis_size("dp")
    grad_scale = float(batch_size * row_count * seq_count * core_count) ** (-0.5)
    offset = lax.axis_index("seq") * row_count
    positions = offset + jnp.arange(row_count, dtype=jnp.int32)
    starts = doc_starts(positions, doc_lengths)
    shallow = min(levels, row_count.bit_length() - 1)
    summed = jnp.zeros(tokens.shape, jnp.float32)
    states = [tokens]
    previous_list = []
    current = tokens
    wide_positions = offset - row_count + jnp.arange(2 * row_count, dtype=jnp.int32)
    wide_starts = doc_starts(wide_positions, doc_lengths)
    wide = jnp.concatenate([shifted_2(tokens, "seq", 1), tokens], axis=1)
    for level_index in range(shallow):
        spacing = 2**level_index
        padding = jnp.zeros((wide.shape[0], spacing, wide.shape[2]), wide.dtype)
        shifted = jnp.concatenate([padding, wide[:, : 2 * row_count - spacing, :]], axis=1)
        previous_wide = jnp.where(
            tap_mask(wide_positions, wide_starts, spacing), shifted, jnp.zeros_like(shifted)
        )
        previous = previous_wide[:, row_count:, :]
        summed = summed + level_weights[level_index] * (
            high_taps[0] * previous + high_taps[1] * current
        )
        wide = (low_taps[0] * previous_wide + low_taps[1] * wide).astype(jnp.bfloat16)
        current = wide[:, row_count:, :]
        previous_list.append(previous)
        states.append(current)
    for level_index in range(shallow, levels):
        spacing = 2**level_index
        device_hops = spacing // row_count
        if device_hops < seq_count:
            shifted = shifted_2(current, "seq", device_hops)
        else:
            shifted = jnp.zeros_like(current)
        previous = jnp.where(tap_mask(positions, starts, spacing), shifted, jnp.zeros_like(shifted))
        summed = summed + level_weights[level_index] * (
            high_taps[0] * previous + high_taps[1] * current
        )
        current = (low_taps[0] * previous + low_taps[1] * current).astype(jnp.bfloat16)
        previous_list.append(previous)
        states.append(current)
    summed = summed + level_weights[levels] * current
    activated = gelu_value(summed).astype(jnp.bfloat16)
    partial_mix = jnp.einsum(
        "brc,oc->bro", activated, mix_weight, preferred_element_type=jnp.float32
    )
    mixed = lax.psum_scatter(
        partial_mix.astype(jnp.bfloat16), "tensor", scatter_dimension=2, tiled=True
    ).astype(jnp.float32)
    result = (tokens.astype(jnp.float32) + mixed).astype(jnp.bfloat16)
    gathered = lax.all_gather(out_grad, "tensor", axis=2, tiled=True)
    act_grad = jnp.einsum("bro,oc->brc", gathered, mix_weight, preferred_element_type=jnp.float32)
    weight_part = (
        jnp.einsum("bro,brc->oc", gathered, activated, preferred_element_type=jnp.float32)
        * grad_scale
    ).astype(jnp.bfloat16)
    weight_part, act_grad = lax.optimization_barrier((weight_part, act_grad))
    weight_grad = lax.psum_scatter(
        weight_part,
        ("seq", "dp"),
        scatter_dimension=0,
        tiled=True,
    )
    summed_grad = act_grad * gelu_slope(summed)
    carry_grad = (level_weights[levels] * summed_grad).astype(jnp.bfloat16)
    weight_sums = [None] * (levels + 1)
    weight_sums[levels] = jnp.sum(summed_grad * states[levels].astype(jnp.float32), axis=(0, 1))
    low_first = jnp.zeros((channels,), jnp.float32)
    low_second = jnp.zeros((channels,), jnp.float32)
    high_first = jnp.zeros((channels,), jnp.float32)
    high_second = jnp.zeros((channels,), jnp.float32)
    next_summed_grad = shifted_2(summed_grad, "seq", -1)
    for level_index in range(levels - 1, shallow - 1, -1):
        spacing = 2**level_index
        current = states[level_index]
        previous = previous_list[level_index]
        weighted = level_weights[level_index] * summed_grad
        highpass = high_taps[0] * previous + high_taps[1] * current
        weight_sums[level_index] = jnp.sum(summed_grad * highpass, axis=(0, 1))
        grad_wide = carry_grad.astype(jnp.float32)
        low_first = low_first + jnp.sum(grad_wide * previous.astype(jnp.float32), axis=(0, 1))
        low_second = low_second + jnp.sum(grad_wide * current.astype(jnp.float32), axis=(0, 1))
        high_first = high_first + jnp.sum(weighted * previous.astype(jnp.float32), axis=(0, 1))
        high_second = high_second + jnp.sum(weighted * current.astype(jnp.float32), axis=(0, 1))
        carried = low_taps[0] * carry_grad + high_taps[0] * weighted
        stayed = low_taps[1] * carry_grad + high_taps[1] * weighted
        outgoing = jnp.where(
            tap_mask(positions, starts, spacing), carried, jnp.zeros_like(carried)
        ).astype(jnp.bfloat16)
        device_hops = spacing // row_count
        if device_hops < seq_count:
            pulled = shifted_2(outgoing, "seq", -device_hops)
        else:
            pulled = jnp.zeros_like(outgoing)
        carry_grad = (stayed + pulled).astype(jnp.bfloat16)
    ahead_positions = offset + jnp.arange(2 * row_count, dtype=jnp.int32)
    ahead_starts = doc_starts(ahead_positions, doc_lengths)
    carry_ahead = jnp.concatenate([carry_grad, shifted_2(carry_grad, "seq", -1)], axis=1)
    summed_grad_ahead = jnp.concatenate([summed_grad, next_summed_grad], axis=1)
    for level_index in range(shallow - 1, -1, -1):
        spacing = 2**level_index
        current = states[level_index]
        previous = previous_list[level_index]
        carry_grad = carry_ahead[:, :row_count, :]
        weighted = level_weights[level_index] * summed_grad
        highpass = high_taps[0] * previous + high_taps[1] * current
        weight_sums[level_index] = jnp.sum(summed_grad * highpass, axis=(0, 1))
        grad_wide = carry_grad.astype(jnp.float32)
        low_first = low_first + jnp.sum(grad_wide * previous.astype(jnp.float32), axis=(0, 1))
        low_second = low_second + jnp.sum(grad_wide * current.astype(jnp.float32), axis=(0, 1))
        high_first = high_first + jnp.sum(weighted * previous.astype(jnp.float32), axis=(0, 1))
        high_second = high_second + jnp.sum(weighted * current.astype(jnp.float32), axis=(0, 1))
        weighted_ahead = level_weights[level_index] * summed_grad_ahead
        carried = low_taps[0] * carry_ahead + high_taps[0] * weighted_ahead
        stayed = low_taps[1] * carry_ahead + high_taps[1] * weighted_ahead
        outgoing = jnp.where(
            tap_mask(ahead_positions, ahead_starts, spacing), carried, jnp.zeros_like(carried)
        ).astype(jnp.bfloat16)
        padding = jnp.zeros((outgoing.shape[0], spacing, outgoing.shape[2]), outgoing.dtype)
        pulled = jnp.concatenate([outgoing[:, spacing:, :], padding], axis=1)
        carry_ahead = (stayed + pulled).astype(jnp.bfloat16)
    carry_grad = carry_ahead[:, :row_count, :]
    token_grad = (out_grad.astype(jnp.float32) + carry_grad.astype(jnp.float32)).astype(
        jnp.bfloat16
    )
    low_grad = jnp.stack([low_first, low_second]) * grad_scale
    high_grad = jnp.stack([high_first, high_second]) * grad_scale
    level_grad = jnp.stack(weight_sums) * grad_scale
    sums = exchange_sum(jnp.concatenate([low_grad, high_grad, level_grad], axis=0), ("dp", "seq"))
    low_grad, high_grad, level_grad = sums[0:2], sums[2:4], sums[4:]
    return (result, token_grad, weight_grad, low_grad, high_grad, level_grad)


def solution(mesh):
    placed = (
        P(("groups", "dp"), "seq", "tensor"),
        P(("groups", "dp"), None),
        P(None, "tensor"),
        P(None, "tensor"),
        P(None, "tensor"),
        P(None, "tensor"),
        P(("groups", "dp"), "seq", "tensor"),
    )
    return jax.shard_map(
        shards,
        mesh=mesh,
        in_specs=placed,
        out_specs=(
            P(("groups", "dp"), "seq", "tensor"),
            P(("groups", "dp"), "seq", "tensor"),
            P(("groups", "seq", "dp"), "tensor"),
            P("groups", "tensor"),
            P("groups", "tensor"),
            P("groups", "tensor"),
        ),
        check_vma=False,
    )
```

```python
import jax
import jax.numpy as jnp
from jax import lax
from jax.sharding import PartitionSpec as P

GELU_SCALE = 0.7978845608028654
GELU_CUBIC = 0.044715


def shifted_2(block, axis, distance):
    devices = range(lax.axis_size(axis))
    route = [(i - distance, i) for i in devices if i - distance in devices]
    return lax.ppermute(block, axis, route)


def exchange_sum(values, axes):
    for axis in axes:
        size = lax.axis_size(axis)
        if size & (size - 1):
            values = lax.psum(values, axis)
            continue
        step = 1
        while step < size:
            route = [(i, i ^ step) for i in range(size)]
            values = values + lax.ppermute(values, axis, route)
            step *= 2
    return values


def gelu_value(values):
    tangent = jnp.tanh(GELU_SCALE * (values + GELU_CUBIC * values * values * values))
    return 0.5 * values * (1.0 + tangent)


def gelu_slope(values):
    tangent = jnp.tanh(GELU_SCALE * (values + GELU_CUBIC * values * values * values))
    return 0.5 * (1.0 + tangent) + 0.5 * values * (1.0 - tangent * tangent) * GELU_SCALE * (
        1.0 + 3.0 * GELU_CUBIC * values * values
    )


def doc_starts(positions, doc_lengths):
    bounds = jnp.cumsum(doc_lengths, axis=1) - doc_lengths
    before = bounds[:, None, :] <= positions[None, :, None]
    return jnp.max(jnp.where(before, bounds[:, None, :], -1), axis=2)


def tap_mask(positions, starts, spacing):
    return (positions[None, :] - spacing >= starts)[:, :, None]


def shards(tokens, doc_lengths, low_taps, high_taps, level_weights, mix_weight, out_grad):
    batch_size, row_count, channels = tokens.shape
    levels = level_weights.shape[0] - 1
    seq_count = lax.axis_size("seq")
    core_count = lax.axis_size("dp")
    grad_scale = float(batch_size * row_count * seq_count * core_count) ** (-0.5)
    offset = lax.axis_index("seq") * row_count
    positions = offset + jnp.arange(row_count, dtype=jnp.int32)
    starts = doc_starts(positions, doc_lengths)
    shallow = min(levels, row_count.bit_length() - 1)
    summed = jnp.zeros(tokens.shape, jnp.float32)
    states = [tokens]
    previous_list = []
    current = tokens
    wide_positions = offset - row_count + jnp.arange(2 * row_count, dtype=jnp.int32)
    wide_starts = doc_starts(wide_positions, doc_lengths)
    wide = jnp.concatenate([shifted_2(tokens, "seq", 1), tokens], axis=1)
    for level_index in range(shallow):
        spacing = 2**level_index
        padding = jnp.zeros((wide.shape[0], spacing, wide.shape[2]), wide.dtype)
        shifted = jnp.concatenate([padding, wide[:, : 2 * row_count - spacing, :]], axis=1)
        previous_wide = jnp.where(
            tap_mask(wide_positions, wide_starts, spacing), shifted, jnp.zeros_like(shifted)
        )
        previous = previous_wide[:, row_count:, :]
        summed = summed + level_weights[level_index] * (
            high_taps[0] * previous + high_taps[1] * current
        )
        wide = (low_taps[0] * previous_wide + low_taps[1] * wide).astype(jnp.bfloat16)
        current = wide[:, row_count:, :]
        previous_list.append(previous)
        states.append(current)
    for level_index in range(shallow, levels):
        spacing = 2**level_index
        device_hops = spacing // row_count
        if device_hops < seq_count:
            shifted = shifted_2(current, "seq", device_hops)
        else:
            shifted = jnp.zeros_like(current)
        previous = jnp.where(tap_mask(positions, starts, spacing), shifted, jnp.zeros_like(shifted))
        summed = summed + level_weights[level_index] * (
            high_taps[0] * previous + high_taps[1] * current
        )
        current = (low_taps[0] * previous + low_taps[1] * current).astype(jnp.bfloat16)
        previous_list.append(previous)
        states.append(current)
    summed = summed + level_weights[levels] * current
    activated = gelu_value(summed).astype(jnp.bfloat16)
    partial_mix = jnp.einsum(
        "brc,oc->bro", activated, mix_weight, preferred_element_type=jnp.float32
    )
    mixed = lax.psum_scatter(
        partial_mix.astype(jnp.bfloat16), "tensor", scatter_dimension=2, tiled=True
    ).astype(jnp.float32)
    result = (tokens.astype(jnp.float32) + mixed).astype(jnp.bfloat16)
    gathered = lax.all_gather(out_grad, "tensor", axis=2, tiled=True)
    act_grad = jnp.einsum("bro,oc->brc", gathered, mix_weight, preferred_element_type=jnp.float32)
    weight_part = (
        jnp.einsum("bro,brc->oc", gathered, activated, preferred_element_type=jnp.float32)
        * grad_scale
    ).astype(jnp.bfloat16)
    weight_part, act_grad = lax.optimization_barrier((weight_part, act_grad))
    summed_grad = act_grad * gelu_slope(summed)
    carry_grad = (level_weights[levels] * summed_grad).astype(jnp.bfloat16)
    weight_sums = [None] * (levels + 1)
    weight_sums[levels] = jnp.sum(summed_grad * states[levels].astype(jnp.float32), axis=(0, 1))
    low_first = jnp.zeros((channels,), jnp.float32)
    low_second = jnp.zeros((channels,), jnp.float32)
    high_first = jnp.zeros((channels,), jnp.float32)
    high_second = jnp.zeros((channels,), jnp.float32)
    for level_index in range(levels - 1, -1, -1):
        if level_index == shallow - 1:
            weight_part, carry_grad = lax.optimization_barrier((weight_part, carry_grad))
            weight_grad = lax.psum_scatter(
                weight_part,
                ("seq", "dp"),
                scatter_dimension=0,
                tiled=True,
            )
        spacing = 2**level_index
        current = states[level_index]
        previous = previous_list[level_index]
        weighted = level_weights[level_index] * summed_grad
        highpass = high_taps[0] * previous + high_taps[1] * current
        weight_sums[level_index] = jnp.sum(summed_grad * highpass, axis=(0, 1))
        grad_wide = carry_grad.astype(jnp.float32)
        low_first = low_first + jnp.sum(grad_wide * previous.astype(jnp.float32), axis=(0, 1))
        low_second = low_second + jnp.sum(grad_wide * current.astype(jnp.float32), axis=(0, 1))
        high_first = high_first + jnp.sum(weighted * previous.astype(jnp.float32), axis=(0, 1))
        high_second = high_second + jnp.sum(weighted * current.astype(jnp.float32), axis=(0, 1))
        carried = low_taps[0] * carry_grad + high_taps[0] * weighted
        stayed = low_taps[1] * carry_grad + high_taps[1] * weighted
        outgoing = jnp.where(
            tap_mask(positions, starts, spacing), carried, jnp.zeros_like(carried)
        ).astype(jnp.bfloat16)
        if level_index < shallow:
            border = shifted_2(outgoing[:, :spacing, :], "seq", -1)
            pulled = jnp.concatenate([outgoing[:, spacing:, :], border], axis=1)
        else:
            device_hops = spacing // row_count
            if device_hops < seq_count:
                pulled = shifted_2(outgoing, "seq", -device_hops)
            else:
                pulled = jnp.zeros_like(outgoing)
        carry_grad = (stayed + pulled).astype(jnp.bfloat16)
    token_grad = (out_grad.astype(jnp.float32) + carry_grad.astype(jnp.float32)).astype(
        jnp.bfloat16
    )
    low_grad = jnp.stack([low_first, low_second]) * grad_scale
    high_grad = jnp.stack([high_first, high_second]) * grad_scale
    level_grad = jnp.stack(weight_sums) * grad_scale
    sums = exchange_sum(jnp.concatenate([low_grad, high_grad, level_grad], axis=0), ("dp", "seq"))
    low_grad, high_grad, level_grad = sums[0:2], sums[2:4], sums[4:]
    return (result, token_grad, weight_grad, low_grad, high_grad, level_grad)


def solution(mesh):
    placed = (
        P(("groups", "dp"), "seq", "tensor"),
        P(("groups", "dp"), None),
        P(None, "tensor"),
        P(None, "tensor"),
        P(None, "tensor"),
        P(None, "tensor"),
        P(("groups", "dp"), "seq", "tensor"),
    )
    return jax.shard_map(
        shards,
        mesh=mesh,
        in_specs=placed,
        out_specs=(
            P(("groups", "dp"), "seq", "tensor"),
            P(("groups", "dp"), "seq", "tensor"),
            P(("groups", "seq", "dp"), "tensor"),
            P("groups", "tensor"),
            P("groups", "tensor"),
            P("groups", "tensor"),
        ),
        check_vma=False,
    )
```

```python
import jax
import jax.numpy as jnp
from jax import lax
from jax.sharding import PartitionSpec as P

GELU_SCALE = 0.7978845608028654
GELU_CUBIC = 0.044715


def shifted_2(block, axis, distance):
    devices = range(lax.axis_size(axis))
    route = [(i - distance, i) for i in devices if i - distance in devices]
    return lax.ppermute(block, axis, route)


def exchange_sum(values, axes):
    for axis in axes:
        size = lax.axis_size(axis)
        if size & (size - 1):
            values = lax.psum(values, axis)
            continue
        step = 1
        while step < size:
            route = [(i, i ^ step) for i in range(size)]
            values = values + lax.ppermute(values, axis, route)
            step *= 2
    return values


def gelu_value(values):
    tangent = jnp.tanh(GELU_SCALE * (values + GELU_CUBIC * values * values * values))
    return 0.5 * values * (1.0 + tangent)


def gelu_slope(values):
    tangent = jnp.tanh(GELU_SCALE * (values + GELU_CUBIC * values * values * values))
    return 0.5 * (1.0 + tangent) + 0.5 * values * (1.0 - tangent * tangent) * GELU_SCALE * (
        1.0 + 3.0 * GELU_CUBIC * values * values
    )


def doc_starts(positions, doc_lengths):
    bounds = jnp.cumsum(doc_lengths, axis=1) - doc_lengths
    before = bounds[:, None, :] <= positions[None, :, None]
    return jnp.max(jnp.where(before, bounds[:, None, :], -1), axis=2)


def tap_mask(positions, starts, spacing):
    return (positions[None, :] - spacing >= starts)[:, :, None]


def shards(tokens, doc_lengths, low_taps, high_taps, level_weights, mix_weight, out_grad):
    batch_size, row_count, channels = tokens.shape
    levels = level_weights.shape[0] - 1
    seq_count = lax.axis_size("seq")
    core_count = lax.axis_size("dp")
    grad_scale = float(batch_size * row_count * seq_count * core_count) ** (-0.5)
    offset = lax.axis_index("seq") * row_count
    positions = offset + jnp.arange(row_count, dtype=jnp.int32)
    starts = doc_starts(positions, doc_lengths)
    shallow = min(levels, row_count.bit_length() - 1)
    summed = jnp.zeros(tokens.shape, jnp.float32)
    states = [tokens]
    previous_list = []
    current = tokens
    wide_positions = offset - row_count + jnp.arange(2 * row_count, dtype=jnp.int32)
    wide_starts = doc_starts(wide_positions, doc_lengths)
    wide = jnp.concatenate([shifted_2(tokens, "seq", 1), tokens], axis=1)
    for level_index in range(shallow):
        spacing = 2**level_index
        padding = jnp.zeros((wide.shape[0], spacing, wide.shape[2]), wide.dtype)
        shifted = jnp.concatenate([padding, wide[:, : 2 * row_count - spacing, :]], axis=1)
        previous_wide = jnp.where(
            tap_mask(wide_positions, wide_starts, spacing), shifted, jnp.zeros_like(shifted)
        )
        previous = previous_wide[:, row_count:, :]
        summed = summed + level_weights[level_index] * (
            high_taps[0] * previous + high_taps[1] * current
        )
        wide = (low_taps[0] * previous_wide + low_taps[1] * wide).astype(jnp.bfloat16)
        current = wide[:, row_count:, :]
        previous_list.append(previous)
        states.append(current)
    for level_index in range(shallow, levels):
        spacing = 2**level_index
        device_hops = spacing // row_count
        if device_hops < seq_count:
            shifted = shifted_2(current, "seq", device_hops)
        else:
            shifted = jnp.zeros_like(current)
        previous = jnp.where(tap_mask(positions, starts, spacing), shifted, jnp.zeros_like(shifted))
        summed = summed + level_weights[level_index] * (
            high_taps[0] * previous + high_taps[1] * current
        )
        current = (low_taps[0] * previous + low_taps[1] * current).astype(jnp.bfloat16)
        previous_list.append(previous)
        states.append(current)
    summed = summed + level_weights[levels] * current
    activated = gelu_value(summed).astype(jnp.bfloat16)
    partial_mix = jnp.einsum(
        "brc,oc->bro", activated, mix_weight, preferred_element_type=jnp.float32
    )
    mixed = lax.psum_scatter(
        partial_mix.astype(jnp.bfloat16), "tensor", scatter_dimension=2, tiled=True
    ).astype(jnp.float32)
    result = (tokens.astype(jnp.float32) + mixed).astype(jnp.bfloat16)
    gathered = lax.all_gather(out_grad, "tensor", axis=2, tiled=True)
    act_grad = jnp.einsum("bro,oc->brc", gathered, mix_weight, preferred_element_type=jnp.float32)
    grad_split = gathered.reshape(
        gathered.shape[:2] + (seq_count, core_count, gathered.shape[2] // (seq_count * core_count))
    )
    weight_part = (
        jnp.einsum("brsdk,brc->dskc", grad_split, activated, preferred_element_type=jnp.float32)
        * grad_scale
    ).astype(jnp.bfloat16)
    weight_part, act_grad = lax.optimization_barrier((weight_part, act_grad))
    weight_part = lax.psum_scatter(weight_part, "dp", scatter_dimension=0, tiled=True)
    summed_grad = act_grad * gelu_slope(summed)
    carry_grad = (level_weights[levels] * summed_grad).astype(jnp.bfloat16)
    weight_sums = [None] * (levels + 1)
    weight_sums[levels] = jnp.sum(summed_grad * states[levels].astype(jnp.float32), axis=(0, 1))
    low_first = jnp.zeros((channels,), jnp.float32)
    low_second = jnp.zeros((channels,), jnp.float32)
    high_first = jnp.zeros((channels,), jnp.float32)
    high_second = jnp.zeros((channels,), jnp.float32)
    for level_index in range(levels - 1, -1, -1):
        if level_index == shallow - 1:
            weight_part, carry_grad = lax.optimization_barrier((weight_part, carry_grad))
            weight_grad = lax.psum_scatter(weight_part, "seq", scatter_dimension=1, tiled=True)
            weight_grad = weight_grad.reshape(weight_grad.shape[2:])
        spacing = 2**level_index
        current = states[level_index]
        previous = previous_list[level_index]
        weighted = level_weights[level_index] * summed_grad
        highpass = high_taps[0] * previous + high_taps[1] * current
        weight_sums[level_index] = jnp.sum(summed_grad * highpass, axis=(0, 1))
        grad_wide = carry_grad.astype(jnp.float32)
        low_first = low_first + jnp.sum(grad_wide * previous.astype(jnp.float32), axis=(0, 1))
        low_second = low_second + jnp.sum(grad_wide * current.astype(jnp.float32), axis=(0, 1))
        high_first = high_first + jnp.sum(weighted * previous.astype(jnp.float32), axis=(0, 1))
        high_second = high_second + jnp.sum(weighted * current.astype(jnp.float32), axis=(0, 1))
        carried = low_taps[0] * carry_grad + high_taps[0] * weighted
        stayed = low_taps[1] * carry_grad + high_taps[1] * weighted
        outgoing = jnp.where(
            tap_mask(positions, starts, spacing), carried, jnp.zeros_like(carried)
        ).astype(jnp.bfloat16)
        if level_index < shallow:
            border = shifted_2(outgoing[:, :spacing, :], "seq", -1)
            pulled = jnp.concatenate([outgoing[:, spacing:, :], border], axis=1)
        else:
            device_hops = spacing // row_count
            if device_hops < seq_count:
                pulled = shifted_2(outgoing, "seq", -device_hops)
            else:
                pulled = jnp.zeros_like(outgoing)
        carry_grad = (stayed + pulled).astype(jnp.bfloat16)
    token_grad = (out_grad.astype(jnp.float32) + carry_grad.astype(jnp.float32)).astype(
        jnp.bfloat16
    )
    low_grad = jnp.stack([low_first, low_second]) * grad_scale
    high_grad = jnp.stack([high_first, high_second]) * grad_scale
    level_grad = jnp.stack(weight_sums) * grad_scale
    sums = exchange_sum(jnp.concatenate([low_grad, high_grad, level_grad], axis=0), ("dp", "seq"))
    low_grad, high_grad, level_grad = sums[0:2], sums[2:4], sums[4:]
    return (result, token_grad, weight_grad, low_grad, high_grad, level_grad)


def solution(mesh):
    placed = (
        P(("groups", "dp"), "seq", "tensor"),
        P(("groups", "dp"), None),
        P(None, "tensor"),
        P(None, "tensor"),
        P(None, "tensor"),
        P(None, "tensor"),
        P(("groups", "dp"), "seq", "tensor"),
    )
    return jax.shard_map(
        shards,
        mesh=mesh,
        in_specs=placed,
        out_specs=(
            P(("groups", "dp"), "seq", "tensor"),
            P(("groups", "dp"), "seq", "tensor"),
            P(("groups", "seq", "dp"), "tensor"),
            P("groups", "tensor"),
            P("groups", "tensor"),
            P("groups", "tensor"),
        ),
        check_vma=False,
    )
```

```python
import jax
import jax.numpy as jnp
from jax import lax
from jax.sharding import PartitionSpec as P

GELU_SCALE = 0.7978845608028654
GELU_CUBIC = 0.044715


def shifted_2(block, axis, distance):
    devices = range(lax.axis_size(axis))
    route = [(i - distance, i) for i in devices if i - distance in devices]
    return lax.ppermute(block, axis, route)


def exchange_sum(values, axes):
    for axis in axes:
        size = lax.axis_size(axis)
        if size & (size - 1):
            values = lax.psum(values, axis)
            continue
        step = 1
        while step < size:
            route = [(i, i ^ step) for i in range(size)]
            values = values + lax.ppermute(values, axis, route)
            step *= 2
    return values


def exchange_scatter(values, axis):
    size = lax.axis_size(axis)
    me = lax.axis_index(axis)
    width = values.shape[-1] // size
    chunks = values.reshape(values.shape[:-1] + (size, width))

    def chunk(index):
        return lax.dynamic_index_in_dim(chunks, index, axis=chunks.ndim - 2, keepdims=False)

    total = chunk(me).astype(jnp.float32)
    for step in range(1, size):
        route = [(i, (i + step) % size) for i in range(size)]
        total = total + lax.ppermute(chunk((me + step) % size), axis, route).astype(jnp.float32)
    return total


def gelu_value(values):
    tangent = jnp.tanh(GELU_SCALE * (values + GELU_CUBIC * values * values * values))
    return 0.5 * values * (1.0 + tangent)


def gelu_slope(values):
    tangent = jnp.tanh(GELU_SCALE * (values + GELU_CUBIC * values * values * values))
    return 0.5 * (1.0 + tangent) + 0.5 * values * (1.0 - tangent * tangent) * GELU_SCALE * (
        1.0 + 3.0 * GELU_CUBIC * values * values
    )


def doc_starts(positions, doc_lengths):
    bounds = jnp.cumsum(doc_lengths, axis=1) - doc_lengths
    before = bounds[:, None, :] <= positions[None, :, None]
    return jnp.max(jnp.where(before, bounds[:, None, :], -1), axis=2)


def tap_mask(positions, starts, spacing):
    return (positions[None, :] - spacing >= starts)[:, :, None]


def shards(tokens, doc_lengths, low_taps, high_taps, level_weights, mix_weight, out_grad):
    batch_size, row_count, channels = tokens.shape
    levels = level_weights.shape[0] - 1
    seq_count = lax.axis_size("seq")
    core_count = lax.axis_size("dp")
    grad_scale = float(batch_size * row_count * seq_count * core_count) ** (-0.5)
    offset = lax.axis_index("seq") * row_count
    positions = offset + jnp.arange(row_count, dtype=jnp.int32)
    starts = doc_starts(positions, doc_lengths)
    shallow = min(levels, row_count.bit_length() - 1)
    summed = jnp.zeros(tokens.shape, jnp.float32)
    states = [tokens]
    previous_list = []
    current = tokens
    wide_positions = offset - row_count + jnp.arange(2 * row_count, dtype=jnp.int32)
    wide_starts = doc_starts(wide_positions, doc_lengths)
    wide = jnp.concatenate([shifted_2(tokens, "seq", 1), tokens], axis=1)
    for level_index in range(shallow):
        spacing = 2**level_index
        padding = jnp.zeros((wide.shape[0], spacing, wide.shape[2]), wide.dtype)
        shifted = jnp.concatenate([padding, wide[:, : 2 * row_count - spacing, :]], axis=1)
        previous_wide = jnp.where(
            tap_mask(wide_positions, wide_starts, spacing), shifted, jnp.zeros_like(shifted)
        )
        previous = previous_wide[:, row_count:, :]
        summed = summed + level_weights[level_index] * (
            high_taps[0] * previous + high_taps[1] * current
        )
        wide = (low_taps[0] * previous_wide + low_taps[1] * wide).astype(jnp.bfloat16)
        current = wide[:, row_count:, :]
        previous_list.append(previous)
        states.append(current)
    for level_index in range(shallow, levels):
        spacing = 2**level_index
        device_hops = spacing // row_count
        if device_hops < seq_count:
            shifted = shifted_2(current, "seq", device_hops)
        else:
            shifted = jnp.zeros_like(current)
        previous = jnp.where(tap_mask(positions, starts, spacing), shifted, jnp.zeros_like(shifted))
        summed = summed + level_weights[level_index] * (
            high_taps[0] * previous + high_taps[1] * current
        )
        current = (low_taps[0] * previous + low_taps[1] * current).astype(jnp.bfloat16)
        previous_list.append(previous)
        states.append(current)
    summed = summed + level_weights[levels] * current
    activated = gelu_value(summed).astype(jnp.bfloat16)
    gathered = lax.all_gather(out_grad, "tensor", axis=2, tiled=True)
    act_grad = jnp.einsum("bro,oc->brc", gathered, mix_weight, preferred_element_type=jnp.float32)
    grad_split = gathered.reshape(
        gathered.shape[:2] + (seq_count, core_count, gathered.shape[2] // (seq_count * core_count))
    )
    weight_part = (
        jnp.einsum("brsdk,brc->dskc", grad_split, activated, preferred_element_type=jnp.float32)
        * grad_scale
    ).astype(jnp.bfloat16)
    weight_part, act_grad = lax.optimization_barrier((weight_part, act_grad))
    weight_part = lax.psum_scatter(weight_part, "dp", scatter_dimension=0, tiled=True)
    summed_grad = act_grad * gelu_slope(summed)
    carry_grad = (level_weights[levels] * summed_grad).astype(jnp.bfloat16)
    weight_sums = [None] * (levels + 1)
    weight_sums[levels] = jnp.sum(summed_grad * states[levels].astype(jnp.float32), axis=(0, 1))
    low_first = jnp.zeros((channels,), jnp.float32)
    low_second = jnp.zeros((channels,), jnp.float32)
    high_first = jnp.zeros((channels,), jnp.float32)
    high_second = jnp.zeros((channels,), jnp.float32)
    for level_index in range(levels - 1, -1, -1):
        if level_index == shallow:
            activated, carry_grad = lax.optimization_barrier((activated, carry_grad))
            partial_mix = jnp.einsum(
                "brc,oc->bro", activated, mix_weight, preferred_element_type=jnp.float32
            )
            mixed = exchange_scatter(partial_mix.astype(jnp.bfloat16), "tensor")
        if level_index == shallow - 1:
            weight_part, carry_grad = lax.optimization_barrier((weight_part, carry_grad))
            weight_grad = lax.psum_scatter(weight_part, "seq", scatter_dimension=1, tiled=True)
            weight_grad = weight_grad.reshape(weight_grad.shape[2:])
        spacing = 2**level_index
        current = states[level_index]
        previous = previous_list[level_index]
        weighted = level_weights[level_index] * summed_grad
        highpass = high_taps[0] * previous + high_taps[1] * current
        weight_sums[level_index] = jnp.sum(summed_grad * highpass, axis=(0, 1))
        grad_wide = carry_grad.astype(jnp.float32)
        low_first = low_first + jnp.sum(grad_wide * previous.astype(jnp.float32), axis=(0, 1))
        low_second = low_second + jnp.sum(grad_wide * current.astype(jnp.float32), axis=(0, 1))
        high_first = high_first + jnp.sum(weighted * previous.astype(jnp.float32), axis=(0, 1))
        high_second = high_second + jnp.sum(weighted * current.astype(jnp.float32), axis=(0, 1))
        carried = low_taps[0] * carry_grad + high_taps[0] * weighted
        stayed = low_taps[1] * carry_grad + high_taps[1] * weighted
        outgoing = jnp.where(
            tap_mask(positions, starts, spacing), carried, jnp.zeros_like(carried)
        ).astype(jnp.bfloat16)
        if level_index < shallow:
            border = shifted_2(outgoing[:, :spacing, :], "seq", -1)
            pulled = jnp.concatenate([outgoing[:, spacing:, :], border], axis=1)
        else:
            device_hops = spacing // row_count
            if device_hops < seq_count:
                pulled = shifted_2(outgoing, "seq", -device_hops)
            else:
                pulled = jnp.zeros_like(outgoing)
        carry_grad = (stayed + pulled).astype(jnp.bfloat16)
    result = (tokens.astype(jnp.float32) + mixed).astype(jnp.bfloat16)
    token_grad = (out_grad.astype(jnp.float32) + carry_grad.astype(jnp.float32)).astype(
        jnp.bfloat16
    )
    low_grad = jnp.stack([low_first, low_second]) * grad_scale
    high_grad = jnp.stack([high_first, high_second]) * grad_scale
    level_grad = jnp.stack(weight_sums) * grad_scale
    sums = exchange_sum(jnp.concatenate([low_grad, high_grad, level_grad], axis=0), ("dp", "seq"))
    low_grad, high_grad, level_grad = sums[0:2], sums[2:4], sums[4:]
    return (result, token_grad, weight_grad, low_grad, high_grad, level_grad)


def solution(mesh):
    placed = (
        P(("groups", "dp"), "seq", "tensor"),
        P(("groups", "dp"), None),
        P(None, "tensor"),
        P(None, "tensor"),
        P(None, "tensor"),
        P(None, "tensor"),
        P(("groups", "dp"), "seq", "tensor"),
    )
    return jax.shard_map(
        shards,
        mesh=mesh,
        in_specs=placed,
        out_specs=(
            P(("groups", "dp"), "seq", "tensor"),
            P(("groups", "dp"), "seq", "tensor"),
            P(("groups", "seq", "dp"), "tensor"),
            P("groups", "tensor"),
            P("groups", "tensor"),
            P("groups", "tensor"),
        ),
        check_vma=False,
    )
```

```python
import jax
import jax.numpy as jnp
from jax import lax
from jax.sharding import PartitionSpec as P

GELU_SCALE = 0.7978845608028654
GELU_CUBIC = 0.044715


def shifted_2(block, axis, distance):
    devices = range(lax.axis_size(axis))
    route = [(i - distance, i) for i in devices if i - distance in devices]
    return lax.ppermute(block, axis, route)


def exchange_sum(values, axes):
    for axis in axes:
        size = lax.axis_size(axis)
        if size & (size - 1):
            values = lax.psum(values, axis)
            continue
        step = 1
        while step < size:
            route = [(i, i ^ step) for i in range(size)]
            values = values + lax.ppermute(values, axis, route)
            step *= 2
    return values


def gelu_value(values):
    tangent = jnp.tanh(GELU_SCALE * (values + GELU_CUBIC * values * values * values))
    return 0.5 * values * (1.0 + tangent)


def gelu_slope(values):
    tangent = jnp.tanh(GELU_SCALE * (values + GELU_CUBIC * values * values * values))
    return 0.5 * (1.0 + tangent) + 0.5 * values * (1.0 - tangent * tangent) * GELU_SCALE * (
        1.0 + 3.0 * GELU_CUBIC * values * values
    )


def doc_starts(positions, doc_lengths):
    bounds = jnp.cumsum(doc_lengths, axis=1) - doc_lengths
    before = bounds[:, None, :] <= positions[None, :, None]
    return jnp.max(jnp.where(before, bounds[:, None, :], -1), axis=2)


def tap_mask(positions, starts, spacing):
    return (positions[None, :] - spacing >= starts)[:, :, None]


def shards(tokens, doc_lengths, low_taps, high_taps, level_weights, mix_weight, out_grad):
    batch_size, row_count, channels = tokens.shape
    levels = level_weights.shape[0] - 1
    seq_count = lax.axis_size("seq")
    core_count = lax.axis_size("dp")
    grad_scale = float(batch_size * row_count * seq_count * core_count) ** (-0.5)
    offset = lax.axis_index("seq") * row_count
    positions = offset + jnp.arange(row_count, dtype=jnp.int32)
    starts = doc_starts(positions, doc_lengths)
    shallow = min(levels, row_count.bit_length() - 1)
    gathered = lax.all_gather(out_grad, "tensor", axis=2, tiled=True)
    share_count = seq_count * core_count
    grad_blocks = jnp.transpose(
        gathered.reshape(row_count, share_count, gathered.shape[2] // share_count), (1, 0, 2)
    )
    grad_rows = lax.all_to_all(grad_blocks, ("seq", "dp"), 0, 0, tiled=True)
    summed = jnp.zeros(tokens.shape, jnp.float32)
    states = [tokens]
    previous_list = []
    current = tokens
    wide_positions = offset - row_count + jnp.arange(2 * row_count, dtype=jnp.int32)
    wide_starts = doc_starts(wide_positions, doc_lengths)
    wide = jnp.concatenate([shifted_2(tokens, "seq", 1), tokens], axis=1)
    for level_index in range(shallow):
        spacing = 2**level_index
        padding = jnp.zeros((wide.shape[0], spacing, wide.shape[2]), wide.dtype)
        shifted = jnp.concatenate([padding, wide[:, : 2 * row_count - spacing, :]], axis=1)
        previous_wide = jnp.where(
            tap_mask(wide_positions, wide_starts, spacing), shifted, jnp.zeros_like(shifted)
        )
        previous = previous_wide[:, row_count:, :]
        summed = summed + level_weights[level_index] * (
            high_taps[0] * previous + high_taps[1] * current
        )
        wide = (low_taps[0] * previous_wide + low_taps[1] * wide).astype(jnp.bfloat16)
        current = wide[:, row_count:, :]
        previous_list.append(previous)
        states.append(current)
    for level_index in range(shallow, levels):
        if level_index == shallow:
            grad_rows, current = lax.optimization_barrier((grad_rows, current))
        spacing = 2**level_index
        device_hops = spacing // row_count
        if device_hops < seq_count:
            shifted = shifted_2(current, "seq", device_hops)
        else:
            shifted = jnp.zeros_like(current)
        previous = jnp.where(tap_mask(positions, starts, spacing), shifted, jnp.zeros_like(shifted))
        summed = summed + level_weights[level_index] * (
            high_taps[0] * previous + high_taps[1] * current
        )
        current = (low_taps[0] * previous + low_taps[1] * current).astype(jnp.bfloat16)
        previous_list.append(previous)
        states.append(current)
    summed = summed + level_weights[levels] * current
    activated = gelu_value(summed).astype(jnp.bfloat16)
    partial_mix = jnp.einsum(
        "brc,oc->bro", activated, mix_weight, preferred_element_type=jnp.float32
    )
    mixed = lax.psum_scatter(
        partial_mix.astype(jnp.bfloat16), "tensor", scatter_dimension=2, tiled=True
    ).astype(jnp.float32)
    result = (tokens.astype(jnp.float32) + mixed).astype(jnp.bfloat16)
    act_grad = jnp.einsum("bro,oc->brc", gathered, mix_weight, preferred_element_type=jnp.float32)
    summed_grad = act_grad * gelu_slope(summed)
    carry_grad = (level_weights[levels] * summed_grad).astype(jnp.bfloat16)
    weight_sums = [None] * (levels + 1)
    weight_sums[levels] = jnp.sum(summed_grad * states[levels].astype(jnp.float32), axis=(0, 1))
    low_first = jnp.zeros((channels,), jnp.float32)
    low_second = jnp.zeros((channels,), jnp.float32)
    high_first = jnp.zeros((channels,), jnp.float32)
    high_second = jnp.zeros((channels,), jnp.float32)
    for level_index in range(levels - 1, -1, -1):
        if level_index == shallow - 1:
            activated, carry_grad = lax.optimization_barrier((activated, carry_grad))
            act_all = lax.all_gather(activated[0], ("seq", "dp"), axis=0, tiled=True)
            weight_grad = (
                jnp.einsum(
                    "to,ti->oi",
                    grad_rows.reshape(-1, grad_rows.shape[2]),
                    act_all,
                    preferred_element_type=jnp.float32,
                )
                * grad_scale
            ).astype(jnp.bfloat16)
        spacing = 2**level_index
        current = states[level_index]
        previous = previous_list[level_index]
        weighted = level_weights[level_index] * summed_grad
        highpass = high_taps[0] * previous + high_taps[1] * current
        weight_sums[level_index] = jnp.sum(summed_grad * highpass, axis=(0, 1))
        grad_wide = carry_grad.astype(jnp.float32)
        low_first = low_first + jnp.sum(grad_wide * previous.astype(jnp.float32), axis=(0, 1))
        low_second = low_second + jnp.sum(grad_wide * current.astype(jnp.float32), axis=(0, 1))
        high_first = high_first + jnp.sum(weighted * previous.astype(jnp.float32), axis=(0, 1))
        high_second = high_second + jnp.sum(weighted * current.astype(jnp.float32), axis=(0, 1))
        carried = low_taps[0] * carry_grad + high_taps[0] * weighted
        stayed = low_taps[1] * carry_grad + high_taps[1] * weighted
        outgoing = jnp.where(
            tap_mask(positions, starts, spacing), carried, jnp.zeros_like(carried)
        ).astype(jnp.bfloat16)
        if level_index < shallow:
            border = shifted_2(outgoing[:, :spacing, :], "seq", -1)
            pulled = jnp.concatenate([outgoing[:, spacing:, :], border], axis=1)
        else:
            device_hops = spacing // row_count
            if device_hops < seq_count:
                pulled = shifted_2(outgoing, "seq", -device_hops)
            else:
                pulled = jnp.zeros_like(outgoing)
        carry_grad = (stayed + pulled).astype(jnp.bfloat16)
    token_grad = (out_grad.astype(jnp.float32) + carry_grad.astype(jnp.float32)).astype(
        jnp.bfloat16
    )
    low_grad = jnp.stack([low_first, low_second]) * grad_scale
    high_grad = jnp.stack([high_first, high_second]) * grad_scale
    level_grad = jnp.stack(weight_sums) * grad_scale
    sums = exchange_sum(jnp.concatenate([low_grad, high_grad, level_grad], axis=0), ("dp", "seq"))
    low_grad, high_grad, level_grad = sums[0:2], sums[2:4], sums[4:]
    return (result, token_grad, weight_grad, low_grad, high_grad, level_grad)


def solution(mesh):
    placed = (
        P(("groups", "dp"), "seq", "tensor"),
        P(("groups", "dp"), None),
        P(None, "tensor"),
        P(None, "tensor"),
        P(None, "tensor"),
        P(None, "tensor"),
        P(("groups", "dp"), "seq", "tensor"),
    )
    return jax.shard_map(
        shards,
        mesh=mesh,
        in_specs=placed,
        out_specs=(
            P(("groups", "dp"), "seq", "tensor"),
            P(("groups", "dp"), "seq", "tensor"),
            P(("groups", "seq", "dp"), "tensor"),
            P("groups", "tensor"),
            P("groups", "tensor"),
            P("groups", "tensor"),
        ),
        check_vma=False,
    )
```

```python
import jax
import jax.numpy as jnp
from jax import lax
from jax.sharding import PartitionSpec as P

GELU_SCALE = 0.7978845608028654
GELU_CUBIC = 0.044715


def shifted_2(block, axis, distance):
    devices = range(lax.axis_size(axis))
    route = [(i - distance, i) for i in devices if i - distance in devices]
    return lax.ppermute(block, axis, route)


def exchange_sum(values, axes):
    for axis in axes:
        size = lax.axis_size(axis)
        if size & (size - 1):
            values = lax.psum(values, axis)
            continue
        step = 1
        while step < size:
            route = [(i, i ^ step) for i in range(size)]
            values = values + lax.ppermute(values, axis, route)
            step *= 2
    return values


def gelu_value(values):
    tangent = jnp.tanh(GELU_SCALE * (values + GELU_CUBIC * values * values * values))
    return 0.5 * values * (1.0 + tangent)


def gelu_slope(values):
    tangent = jnp.tanh(GELU_SCALE * (values + GELU_CUBIC * values * values * values))
    return 0.5 * (1.0 + tangent) + 0.5 * values * (1.0 - tangent * tangent) * GELU_SCALE * (
        1.0 + 3.0 * GELU_CUBIC * values * values
    )


def doc_starts(positions, doc_lengths):
    bounds = jnp.cumsum(doc_lengths, axis=1) - doc_lengths
    before = bounds[:, None, :] <= positions[None, :, None]
    return jnp.max(jnp.where(before, bounds[:, None, :], -1), axis=2)


def tap_mask(positions, starts, spacing):
    return (positions[None, :] - spacing >= starts)[:, :, None]


def shards(tokens, doc_lengths, low_taps, high_taps, level_weights, mix_weight, out_grad):
    batch_size, row_count, channels = tokens.shape
    levels = level_weights.shape[0] - 1
    seq_count = lax.axis_size("seq")
    core_count = lax.axis_size("dp")
    grad_scale = float(batch_size * row_count * seq_count * core_count) ** (-0.5)
    offset = lax.axis_index("seq") * row_count
    positions = offset + jnp.arange(row_count, dtype=jnp.int32)
    starts = doc_starts(positions, doc_lengths)
    shallow = min(levels, row_count.bit_length() - 1)
    gathered = lax.all_gather(out_grad, "tensor", axis=2, tiled=True)
    share_count = seq_count * core_count
    grad_blocks = jnp.transpose(
        gathered.reshape(row_count, share_count, gathered.shape[2] // share_count), (1, 0, 2)
    )
    grad_rows = lax.all_to_all(grad_blocks, ("seq", "dp"), 0, 0, tiled=True)
    summed = jnp.zeros(tokens.shape, jnp.float32)
    states = [tokens]
    previous_list = []
    current = tokens
    wide_positions = offset - row_count + jnp.arange(2 * row_count, dtype=jnp.int32)
    wide_starts = doc_starts(wide_positions, doc_lengths)
    wide = jnp.concatenate([shifted_2(tokens, "seq", 1), tokens], axis=1)
    for level_index in range(shallow):
        spacing = 2**level_index
        padding = jnp.zeros((wide.shape[0], spacing, wide.shape[2]), wide.dtype)
        shifted = jnp.concatenate([padding, wide[:, : 2 * row_count - spacing, :]], axis=1)
        previous_wide = jnp.where(
            tap_mask(wide_positions, wide_starts, spacing), shifted, jnp.zeros_like(shifted)
        )
        previous = previous_wide[:, row_count:, :]
        summed = summed + level_weights[level_index] * (
            high_taps[0] * previous + high_taps[1] * current
        )
        wide = (low_taps[0] * previous_wide + low_taps[1] * wide).astype(jnp.bfloat16)
        current = wide[:, row_count:, :]
        previous_list.append(previous)
        states.append(current)
    for level_index in range(shallow, levels):
        spacing = 2**level_index
        device_hops = spacing // row_count
        if device_hops < seq_count:
            shifted = shifted_2(current, "seq", device_hops)
        else:
            shifted = jnp.zeros_like(current)
        previous = jnp.where(tap_mask(positions, starts, spacing), shifted, jnp.zeros_like(shifted))
        summed = summed + level_weights[level_index] * (
            high_taps[0] * previous + high_taps[1] * current
        )
        current = (low_taps[0] * previous + low_taps[1] * current).astype(jnp.bfloat16)
        previous_list.append(previous)
        states.append(current)
    summed = summed + level_weights[levels] * current
    activated = gelu_value(summed).astype(jnp.bfloat16)
    partial_mix = jnp.einsum(
        "brc,oc->bro", activated, mix_weight, preferred_element_type=jnp.float32
    )
    mixed = lax.psum_scatter(
        partial_mix.astype(jnp.bfloat16), "tensor", scatter_dimension=2, tiled=True
    ).astype(jnp.float32)
    result = (tokens.astype(jnp.float32) + mixed).astype(jnp.bfloat16)
    act_grad = jnp.einsum("bro,oc->brc", gathered, mix_weight, preferred_element_type=jnp.float32)
    summed_grad = act_grad * gelu_slope(summed)
    carry_grad = (level_weights[levels] * summed_grad).astype(jnp.bfloat16)
    weight_sums = [None] * (levels + 1)
    weight_sums[levels] = jnp.sum(summed_grad * states[levels].astype(jnp.float32), axis=(0, 1))
    low_first = jnp.zeros((channels,), jnp.float32)
    low_second = jnp.zeros((channels,), jnp.float32)
    high_first = jnp.zeros((channels,), jnp.float32)
    high_second = jnp.zeros((channels,), jnp.float32)
    for level_index in range(levels - 1, -1, -1):
        if level_index == shallow:
            grad_rows, carry_grad = lax.optimization_barrier((grad_rows, carry_grad))
        if level_index == shallow - 1:
            activated, carry_grad = lax.optimization_barrier((activated, carry_grad))
            act_all = lax.all_gather(activated[0], ("seq", "dp"), axis=0, tiled=True)
            weight_grad = (
                jnp.einsum(
                    "to,ti->oi",
                    grad_rows.reshape(-1, grad_rows.shape[2]),
                    act_all,
                    preferred_element_type=jnp.float32,
                )
                * grad_scale
            ).astype(jnp.bfloat16)
        spacing = 2**level_index
        current = states[level_index]
        previous = previous_list[level_index]
        weighted = level_weights[level_index] * summed_grad
        highpass = high_taps[0] * previous + high_taps[1] * current
        weight_sums[level_index] = jnp.sum(summed_grad * highpass, axis=(0, 1))
        grad_wide = carry_grad.astype(jnp.float32)
        low_first = low_first + jnp.sum(grad_wide * previous.astype(jnp.float32), axis=(0, 1))
        low_second = low_second + jnp.sum(grad_wide * current.astype(jnp.float32), axis=(0, 1))
        high_first = high_first + jnp.sum(weighted * previous.astype(jnp.float32), axis=(0, 1))
        high_second = high_second + jnp.sum(weighted * current.astype(jnp.float32), axis=(0, 1))
        carried = low_taps[0] * carry_grad + high_taps[0] * weighted
        stayed = low_taps[1] * carry_grad + high_taps[1] * weighted
        outgoing = jnp.where(
            tap_mask(positions, starts, spacing), carried, jnp.zeros_like(carried)
        ).astype(jnp.bfloat16)
        if level_index < shallow:
            border = shifted_2(outgoing[:, :spacing, :], "seq", -1)
            pulled = jnp.concatenate([outgoing[:, spacing:, :], border], axis=1)
        else:
            device_hops = spacing // row_count
            if device_hops < seq_count:
                pulled = shifted_2(outgoing, "seq", -device_hops)
            else:
                pulled = jnp.zeros_like(outgoing)
        carry_grad = (stayed + pulled).astype(jnp.bfloat16)
    token_grad = (out_grad.astype(jnp.float32) + carry_grad.astype(jnp.float32)).astype(
        jnp.bfloat16
    )
    low_grad = jnp.stack([low_first, low_second]) * grad_scale
    high_grad = jnp.stack([high_first, high_second]) * grad_scale
    level_grad = jnp.stack(weight_sums) * grad_scale
    sums = exchange_sum(jnp.concatenate([low_grad, high_grad, level_grad], axis=0), ("dp", "seq"))
    low_grad, high_grad, level_grad = sums[0:2], sums[2:4], sums[4:]
    return (result, token_grad, weight_grad, low_grad, high_grad, level_grad)


def solution(mesh):
    placed = (
        P(("groups", "dp"), "seq", "tensor"),
        P(("groups", "dp"), None),
        P(None, "tensor"),
        P(None, "tensor"),
        P(None, "tensor"),
        P(None, "tensor"),
        P(("groups", "dp"), "seq", "tensor"),
    )
    return jax.shard_map(
        shards,
        mesh=mesh,
        in_specs=placed,
        out_specs=(
            P(("groups", "dp"), "seq", "tensor"),
            P(("groups", "dp"), "seq", "tensor"),
            P(("groups", "seq", "dp"), "tensor"),
            P("groups", "tensor"),
            P("groups", "tensor"),
            P("groups", "tensor"),
        ),
        check_vma=False,
    )
```

```python
import jax
import jax.numpy as jnp
from jax import lax
from jax.sharding import PartitionSpec as P

GELU_SCALE = 0.7978845608028654
GELU_CUBIC = 0.044715


def shifted_2(block, axis, distance):
    devices = range(lax.axis_size(axis))
    route = [(i - distance, i) for i in devices if i - distance in devices]
    return lax.ppermute(block, axis, route)


def exchange_sum(values, axes):
    for axis in axes:
        size = lax.axis_size(axis)
        if size & (size - 1):
            values = lax.psum(values, axis)
            continue
        step = 1
        while step < size:
            route = [(i, i ^ step) for i in range(size)]
            values = values + lax.ppermute(values, axis, route)
            step *= 2
    return values


def gelu_value(values):
    tangent = jnp.tanh(GELU_SCALE * (values + GELU_CUBIC * values * values * values))
    return 0.5 * values * (1.0 + tangent)


def gelu_slope(values):
    tangent = jnp.tanh(GELU_SCALE * (values + GELU_CUBIC * values * values * values))
    return 0.5 * (1.0 + tangent) + 0.5 * values * (1.0 - tangent * tangent) * GELU_SCALE * (
        1.0 + 3.0 * GELU_CUBIC * values * values
    )


def doc_starts(positions, doc_lengths):
    bounds = jnp.cumsum(doc_lengths, axis=1) - doc_lengths
    before = bounds[:, None, :] <= positions[None, :, None]
    return jnp.max(jnp.where(before, bounds[:, None, :], -1), axis=2)


def tap_mask(positions, starts, spacing):
    return (positions[None, :] - spacing >= starts)[:, :, None]


def shards(tokens, doc_lengths, low_taps, high_taps, level_weights, mix_weight, out_grad):
    batch_size, row_count, channels = tokens.shape
    levels = level_weights.shape[0] - 1
    seq_count = lax.axis_size("seq")
    core_count = lax.axis_size("dp")
    grad_scale = float(batch_size * row_count * seq_count * core_count) ** (-0.5)
    offset = lax.axis_index("seq") * row_count
    positions = offset + jnp.arange(row_count, dtype=jnp.int32)
    starts = doc_starts(positions, doc_lengths)
    shallow = min(levels, row_count.bit_length() - 1)
    gathered = lax.all_gather(out_grad, "tensor", axis=2, tiled=True)
    share_count = seq_count * core_count
    grad_blocks = jnp.transpose(
        gathered.reshape(row_count, share_count, gathered.shape[2] // share_count), (1, 0, 2)
    )
    grad_rows = lax.all_to_all(grad_blocks, ("seq", "dp"), 0, 0, tiled=True)
    summed = jnp.zeros(tokens.shape, jnp.float32)
    states = [tokens]
    previous_list = []
    current = tokens
    wide_positions = offset - row_count + jnp.arange(2 * row_count, dtype=jnp.int32)
    wide_starts = doc_starts(wide_positions, doc_lengths)
    wide = jnp.concatenate([shifted_2(tokens, "seq", 1), tokens], axis=1)
    for level_index in range(shallow):
        spacing = 2**level_index
        padding = jnp.zeros((wide.shape[0], spacing, wide.shape[2]), wide.dtype)
        shifted = jnp.concatenate([padding, wide[:, : 2 * row_count - spacing, :]], axis=1)
        previous_wide = jnp.where(
            tap_mask(wide_positions, wide_starts, spacing), shifted, jnp.zeros_like(shifted)
        )
        previous = previous_wide[:, row_count:, :]
        summed = summed + level_weights[level_index] * (
            high_taps[0] * previous + high_taps[1] * current
        )
        wide = (low_taps[0] * previous_wide + low_taps[1] * wide).astype(jnp.bfloat16)
        current = wide[:, row_count:, :]
        previous_list.append(previous)
        states.append(current)
    for level_index in range(shallow, levels):
        spacing = 2**level_index
        device_hops = spacing // row_count
        if device_hops < seq_count:
            shifted = shifted_2(current, "seq", device_hops)
        else:
            shifted = jnp.zeros_like(current)
        previous = jnp.where(tap_mask(positions, starts, spacing), shifted, jnp.zeros_like(shifted))
        summed = summed + level_weights[level_index] * (
            high_taps[0] * previous + high_taps[1] * current
        )
        current = (low_taps[0] * previous + low_taps[1] * current).astype(jnp.bfloat16)
        previous_list.append(previous)
        states.append(current)
    summed = summed + level_weights[levels] * current
    activated = gelu_value(summed).astype(jnp.bfloat16)
    partial_mix = jnp.einsum(
        "brc,oc->bro", activated, mix_weight, preferred_element_type=jnp.float32
    )
    mixed = lax.psum_scatter(
        partial_mix.astype(jnp.bfloat16), "tensor", scatter_dimension=2, tiled=True
    ).astype(jnp.float32)
    result = (tokens.astype(jnp.float32) + mixed).astype(jnp.bfloat16)
    act_grad = jnp.einsum("bro,oc->brc", gathered, mix_weight, preferred_element_type=jnp.float32)
    summed_grad = act_grad * gelu_slope(summed)
    carry_grad = (level_weights[levels] * summed_grad).astype(jnp.bfloat16)
    weight_sums = [None] * (levels + 1)
    weight_sums[levels] = jnp.sum(summed_grad * states[levels].astype(jnp.float32), axis=(0, 1))
    low_first = jnp.zeros((channels,), jnp.float32)
    low_second = jnp.zeros((channels,), jnp.float32)
    high_first = jnp.zeros((channels,), jnp.float32)
    high_second = jnp.zeros((channels,), jnp.float32)
    for level_index in range(levels - 1, -1, -1):
        if level_index == levels - 1:
            grad_rows, carry_grad = lax.optimization_barrier((grad_rows, carry_grad))
        if level_index == shallow - 1:
            activated, carry_grad = lax.optimization_barrier((activated, carry_grad))
            act_all = lax.all_gather(activated[0], ("seq", "dp"), axis=0, tiled=True)
            weight_grad = (
                jnp.einsum(
                    "to,ti->oi",
                    grad_rows.reshape(-1, grad_rows.shape[2]),
                    act_all,
                    preferred_element_type=jnp.float32,
                )
                * grad_scale
            ).astype(jnp.bfloat16)
        spacing = 2**level_index
        current = states[level_index]
        previous = previous_list[level_index]
        weighted = level_weights[level_index] * summed_grad
        highpass = high_taps[0] * previous + high_taps[1] * current
        weight_sums[level_index] = jnp.sum(summed_grad * highpass, axis=(0, 1))
        grad_wide = carry_grad.astype(jnp.float32)
        low_first = low_first + jnp.sum(grad_wide * previous.astype(jnp.float32), axis=(0, 1))
        low_second = low_second + jnp.sum(grad_wide * current.astype(jnp.float32), axis=(0, 1))
        high_first = high_first + jnp.sum(weighted * previous.astype(jnp.float32), axis=(0, 1))
        high_second = high_second + jnp.sum(weighted * current.astype(jnp.float32), axis=(0, 1))
        carried = low_taps[0] * carry_grad + high_taps[0] * weighted
        stayed = low_taps[1] * carry_grad + high_taps[1] * weighted
        outgoing = jnp.where(
            tap_mask(positions, starts, spacing), carried, jnp.zeros_like(carried)
        ).astype(jnp.bfloat16)
        if level_index < shallow:
            border = shifted_2(outgoing[:, :spacing, :], "seq", -1)
            pulled = jnp.concatenate([outgoing[:, spacing:, :], border], axis=1)
        else:
            device_hops = spacing // row_count
            if device_hops < seq_count:
                pulled = shifted_2(outgoing, "seq", -device_hops)
            else:
                pulled = jnp.zeros_like(outgoing)
        carry_grad = (stayed + pulled).astype(jnp.bfloat16)
    token_grad = (out_grad.astype(jnp.float32) + carry_grad.astype(jnp.float32)).astype(
        jnp.bfloat16
    )
    low_grad = jnp.stack([low_first, low_second]) * grad_scale
    high_grad = jnp.stack([high_first, high_second]) * grad_scale
    level_grad = jnp.stack(weight_sums) * grad_scale
    sums = exchange_sum(jnp.concatenate([low_grad, high_grad, level_grad], axis=0), ("dp", "seq"))
    low_grad, high_grad, level_grad = sums[0:2], sums[2:4], sums[4:]
    return (result, token_grad, weight_grad, low_grad, high_grad, level_grad)


def solution(mesh):
    placed = (
        P(("groups", "dp"), "seq", "tensor"),
        P(("groups", "dp"), None),
        P(None, "tensor"),
        P(None, "tensor"),
        P(None, "tensor"),
        P(None, "tensor"),
        P(("groups", "dp"), "seq", "tensor"),
    )
    return jax.shard_map(
        shards,
        mesh=mesh,
        in_specs=placed,
        out_specs=(
            P(("groups", "dp"), "seq", "tensor"),
            P(("groups", "dp"), "seq", "tensor"),
            P(("groups", "seq", "dp"), "tensor"),
            P("groups", "tensor"),
            P("groups", "tensor"),
            P("groups", "tensor"),
        ),
        check_vma=False,
    )
```

```python
import jax
import jax.numpy as jnp
from jax import lax
from jax.sharding import PartitionSpec as P

GELU_SCALE = 0.7978845608028654
GELU_CUBIC = 0.044715


def shifted_2(block, axis, distance):
    devices = range(lax.axis_size(axis))
    route = [(i - distance, i) for i in devices if i - distance in devices]
    return lax.ppermute(block, axis, route)


def exchange_sum(values, axes):
    for axis in axes:
        size = lax.axis_size(axis)
        if size & (size - 1):
            values = lax.psum(values, axis)
            continue
        step = 1
        while step < size:
            route = [(i, i ^ step) for i in range(size)]
            values = values + lax.ppermute(values, axis, route)
            step *= 2
    return values


def gelu_value(values):
    tangent = jnp.tanh(GELU_SCALE * (values + GELU_CUBIC * values * values * values))
    return 0.5 * values * (1.0 + tangent)


def gelu_slope(values):
    tangent = jnp.tanh(GELU_SCALE * (values + GELU_CUBIC * values * values * values))
    return 0.5 * (1.0 + tangent) + 0.5 * values * (1.0 - tangent * tangent) * GELU_SCALE * (
        1.0 + 3.0 * GELU_CUBIC * values * values
    )


def doc_starts(positions, doc_lengths):
    bounds = jnp.cumsum(doc_lengths, axis=1) - doc_lengths
    before = bounds[:, None, :] <= positions[None, :, None]
    return jnp.max(jnp.where(before, bounds[:, None, :], -1), axis=2)


def tap_mask(positions, starts, spacing):
    return (positions[None, :] - spacing >= starts)[:, :, None]


def shards(tokens, doc_lengths, low_taps, high_taps, level_weights, mix_weight, out_grad):
    batch_size, row_count, channels = tokens.shape
    levels = level_weights.shape[0] - 1
    seq_count = lax.axis_size("seq")
    core_count = lax.axis_size("dp")
    grad_scale = float(batch_size * row_count * seq_count * core_count) ** (-0.5)
    offset = lax.axis_index("seq") * row_count
    positions = offset + jnp.arange(row_count, dtype=jnp.int32)
    starts = doc_starts(positions, doc_lengths)
    shallow = min(levels, row_count.bit_length() - 1)
    gathered = lax.all_gather(out_grad, "tensor", axis=2, tiled=True)
    share_count = seq_count * core_count
    grad_blocks = jnp.transpose(
        gathered.reshape(row_count, share_count, gathered.shape[2] // share_count), (1, 0, 2)
    )
    grad_rows = lax.all_to_all(grad_blocks, ("seq", "dp"), 0, 0, tiled=True)
    summed = jnp.zeros(tokens.shape, jnp.float32)
    states = [tokens]
    previous_list = []
    current = tokens
    wide_positions = offset - row_count + jnp.arange(2 * row_count, dtype=jnp.int32)
    wide_starts = doc_starts(wide_positions, doc_lengths)
    wide = jnp.concatenate([shifted_2(tokens, "seq", 1), tokens], axis=1)
    for level_index in range(shallow):
        spacing = 2**level_index
        padding = jnp.zeros((wide.shape[0], spacing, wide.shape[2]), wide.dtype)
        shifted = jnp.concatenate([padding, wide[:, : 2 * row_count - spacing, :]], axis=1)
        previous_wide = jnp.where(
            tap_mask(wide_positions, wide_starts, spacing), shifted, jnp.zeros_like(shifted)
        )
        previous = previous_wide[:, row_count:, :]
        summed = summed + level_weights[level_index] * (
            high_taps[0] * previous + high_taps[1] * current
        )
        wide = (low_taps[0] * previous_wide + low_taps[1] * wide).astype(jnp.bfloat16)
        current = wide[:, row_count:, :]
        previous_list.append(previous)
        states.append(current)
    for level_index in range(shallow, levels):
        spacing = 2**level_index
        device_hops = spacing // row_count
        if device_hops < seq_count:
            shifted = shifted_2(current, "seq", device_hops)
        else:
            shifted = jnp.zeros_like(current)
        previous = jnp.where(tap_mask(positions, starts, spacing), shifted, jnp.zeros_like(shifted))
        summed = summed + level_weights[level_index] * (
            high_taps[0] * previous + high_taps[1] * current
        )
        current = (low_taps[0] * previous + low_taps[1] * current).astype(jnp.bfloat16)
        previous_list.append(previous)
        states.append(current)
    summed = summed + level_weights[levels] * current
    activated = gelu_value(summed).astype(jnp.bfloat16)
    partial_mix = jnp.einsum(
        "brc,oc->bro", activated, mix_weight, preferred_element_type=jnp.float32
    )
    mixed = lax.psum_scatter(
        partial_mix.astype(jnp.bfloat16), "tensor", scatter_dimension=2, tiled=True
    ).astype(jnp.float32)
    result = (tokens.astype(jnp.float32) + mixed).astype(jnp.bfloat16)
    act_grad = jnp.einsum("bro,oc->brc", gathered, mix_weight, preferred_element_type=jnp.float32)
    summed_grad = act_grad * gelu_slope(summed)
    carry_grad = (level_weights[levels] * summed_grad).astype(jnp.bfloat16)
    weight_sums = [None] * (levels + 1)
    weight_sums[levels] = jnp.sum(summed_grad * states[levels].astype(jnp.float32), axis=(0, 1))
    low_first = jnp.zeros((channels,), jnp.float32)
    low_second = jnp.zeros((channels,), jnp.float32)
    high_first = jnp.zeros((channels,), jnp.float32)
    high_second = jnp.zeros((channels,), jnp.float32)
    for level_index in range(levels - 1, -1, -1):
        if level_index == shallow:
            grad_rows, carry_grad = lax.optimization_barrier((grad_rows, carry_grad))
        if level_index == shallow - 1:
            activated, carry_grad = lax.optimization_barrier((activated, carry_grad))
            act_all = lax.all_gather(activated[0], ("seq", "dp"), axis=0, tiled=True)
            weight_grad = (
                jnp.einsum(
                    "to,ti->oi",
                    grad_rows.reshape(-1, grad_rows.shape[2]),
                    act_all,
                    preferred_element_type=jnp.float32,
                )
                * grad_scale
            ).astype(jnp.bfloat16)
        if level_index == 0:
            weight_grad, carry_grad = lax.optimization_barrier((weight_grad, carry_grad))
        spacing = 2**level_index
        current = states[level_index]
        previous = previous_list[level_index]
        weighted = level_weights[level_index] * summed_grad
        highpass = high_taps[0] * previous + high_taps[1] * current
        weight_sums[level_index] = jnp.sum(summed_grad * highpass, axis=(0, 1))
        grad_wide = carry_grad.astype(jnp.float32)
        low_first = low_first + jnp.sum(grad_wide * previous.astype(jnp.float32), axis=(0, 1))
        low_second = low_second + jnp.sum(grad_wide * current.astype(jnp.float32), axis=(0, 1))
        high_first = high_first + jnp.sum(weighted * previous.astype(jnp.float32), axis=(0, 1))
        high_second = high_second + jnp.sum(weighted * current.astype(jnp.float32), axis=(0, 1))
        carried = low_taps[0] * carry_grad + high_taps[0] * weighted
        stayed = low_taps[1] * carry_grad + high_taps[1] * weighted
        outgoing = jnp.where(
            tap_mask(positions, starts, spacing), carried, jnp.zeros_like(carried)
        ).astype(jnp.bfloat16)
        if level_index < shallow:
            border = shifted_2(outgoing[:, :spacing, :], "seq", -1)
            pulled = jnp.concatenate([outgoing[:, spacing:, :], border], axis=1)
        else:
            device_hops = spacing // row_count
            if device_hops < seq_count:
                pulled = shifted_2(outgoing, "seq", -device_hops)
            else:
                pulled = jnp.zeros_like(outgoing)
        carry_grad = (stayed + pulled).astype(jnp.bfloat16)
    token_grad = (out_grad.astype(jnp.float32) + carry_grad.astype(jnp.float32)).astype(
        jnp.bfloat16
    )
    low_grad = jnp.stack([low_first, low_second]) * grad_scale
    high_grad = jnp.stack([high_first, high_second]) * grad_scale
    level_grad = jnp.stack(weight_sums) * grad_scale
    sums = exchange_sum(jnp.concatenate([low_grad, high_grad, level_grad], axis=0), ("dp", "seq"))
    low_grad, high_grad, level_grad = sums[0:2], sums[2:4], sums[4:]
    return (result, token_grad, weight_grad, low_grad, high_grad, level_grad)


def solution(mesh):
    placed = (
        P(("groups", "dp"), "seq", "tensor"),
        P(("groups", "dp"), None),
        P(None, "tensor"),
        P(None, "tensor"),
        P(None, "tensor"),
        P(None, "tensor"),
        P(("groups", "dp"), "seq", "tensor"),
    )
    return jax.shard_map(
        shards,
        mesh=mesh,
        in_specs=placed,
        out_specs=(
            P(("groups", "dp"), "seq", "tensor"),
            P(("groups", "dp"), "seq", "tensor"),
            P(("groups", "seq", "dp"), "tensor"),
            P("groups", "tensor"),
            P("groups", "tensor"),
            P("groups", "tensor"),
        ),
        check_vma=False,
    )
```

```python
import jax
import jax.numpy as jnp
from jax import lax
from jax.sharding import PartitionSpec as P

GELU_SCALE = 0.7978845608028654
GELU_CUBIC = 0.044715


def shifted_2(block, axis, distance):
    devices = range(lax.axis_size(axis))
    route = [(i - distance, i) for i in devices if i - distance in devices]
    return lax.ppermute(block, axis, route)


def exchange_sum(values, axes):
    for axis in axes:
        size = lax.axis_size(axis)
        if size & (size - 1):
            values = lax.psum(values, axis)
            continue
        step = 1
        while step < size:
            route = [(i, i ^ step) for i in range(size)]
            values = values + lax.ppermute(values, axis, route)
            step *= 2
    return values


def exchange_scatter(values, axis):
    size = lax.axis_size(axis)
    me = lax.axis_index(axis)
    width = values.shape[-1] // size
    chunks = values.reshape(values.shape[:-1] + (size, width))

    def chunk(index):
        return lax.dynamic_index_in_dim(chunks, index, axis=chunks.ndim - 2, keepdims=False)

    total = chunk(me).astype(jnp.float32)
    for step in range(1, size):
        route = [(i, (i + step) % size) for i in range(size)]
        total = total + lax.ppermute(chunk((me + step) % size), axis, route).astype(jnp.float32)
    return total


def gelu_value(values):
    tangent = jnp.tanh(GELU_SCALE * (values + GELU_CUBIC * values * values * values))
    return 0.5 * values * (1.0 + tangent)


def gelu_slope(values):
    tangent = jnp.tanh(GELU_SCALE * (values + GELU_CUBIC * values * values * values))
    return 0.5 * (1.0 + tangent) + 0.5 * values * (1.0 - tangent * tangent) * GELU_SCALE * (
        1.0 + 3.0 * GELU_CUBIC * values * values
    )


def doc_starts(positions, doc_lengths):
    bounds = jnp.cumsum(doc_lengths, axis=1) - doc_lengths
    before = bounds[:, None, :] <= positions[None, :, None]
    return jnp.max(jnp.where(before, bounds[:, None, :], -1), axis=2)


def tap_mask(positions, starts, spacing):
    return (positions[None, :] - spacing >= starts)[:, :, None]


def shards(tokens, doc_lengths, low_taps, high_taps, level_weights, mix_weight, out_grad):
    batch_size, row_count, channels = tokens.shape
    levels = level_weights.shape[0] - 1
    seq_count = lax.axis_size("seq")
    core_count = lax.axis_size("dp")
    grad_scale = float(batch_size * row_count * seq_count * core_count) ** (-0.5)
    offset = lax.axis_index("seq") * row_count
    positions = offset + jnp.arange(row_count, dtype=jnp.int32)
    starts = doc_starts(positions, doc_lengths)
    shallow = min(levels, row_count.bit_length() - 1)
    gathered = lax.all_gather(out_grad, "tensor", axis=2, tiled=True)
    share_count = seq_count * core_count
    grad_blocks = jnp.transpose(
        gathered.reshape(row_count, share_count, gathered.shape[2] // share_count), (1, 0, 2)
    )
    grad_rows = lax.all_to_all(grad_blocks, ("seq", "dp"), 0, 0, tiled=True)
    summed = jnp.zeros(tokens.shape, jnp.float32)
    states = [tokens]
    previous_list = []
    current = tokens
    wide_positions = offset - row_count + jnp.arange(2 * row_count, dtype=jnp.int32)
    wide_starts = doc_starts(wide_positions, doc_lengths)
    wide = jnp.concatenate([shifted_2(tokens, "seq", 1), tokens], axis=1)
    for level_index in range(shallow):
        spacing = 2**level_index
        padding = jnp.zeros((wide.shape[0], spacing, wide.shape[2]), wide.dtype)
        shifted = jnp.concatenate([padding, wide[:, : 2 * row_count - spacing, :]], axis=1)
        previous_wide = jnp.where(
            tap_mask(wide_positions, wide_starts, spacing), shifted, jnp.zeros_like(shifted)
        )
        previous = previous_wide[:, row_count:, :]
        summed = summed + level_weights[level_index] * (
            high_taps[0] * previous + high_taps[1] * current
        )
        wide = (low_taps[0] * previous_wide + low_taps[1] * wide).astype(jnp.bfloat16)
        current = wide[:, row_count:, :]
        previous_list.append(previous)
        states.append(current)
    for level_index in range(shallow, levels):
        spacing = 2**level_index
        device_hops = spacing // row_count
        if device_hops < seq_count:
            shifted = shifted_2(current, "seq", device_hops)
        else:
            shifted = jnp.zeros_like(current)
        previous = jnp.where(tap_mask(positions, starts, spacing), shifted, jnp.zeros_like(shifted))
        summed = summed + level_weights[level_index] * (
            high_taps[0] * previous + high_taps[1] * current
        )
        current = (low_taps[0] * previous + low_taps[1] * current).astype(jnp.bfloat16)
        previous_list.append(previous)
        states.append(current)
    summed = summed + level_weights[levels] * current
    activated = gelu_value(summed).astype(jnp.bfloat16)
    partial_mix = jnp.einsum(
        "brc,oc->bro", activated, mix_weight, preferred_element_type=jnp.float32
    )
    mixed = exchange_scatter(partial_mix.astype(jnp.bfloat16), "tensor")
    result = (tokens.astype(jnp.float32) + mixed).astype(jnp.bfloat16)
    act_grad = jnp.einsum("bro,oc->brc", gathered, mix_weight, preferred_element_type=jnp.float32)
    summed_grad = act_grad * gelu_slope(summed)
    carry_grad = (level_weights[levels] * summed_grad).astype(jnp.bfloat16)
    weight_sums = [None] * (levels + 1)
    weight_sums[levels] = jnp.sum(summed_grad * states[levels].astype(jnp.float32), axis=(0, 1))
    low_first = jnp.zeros((channels,), jnp.float32)
    low_second = jnp.zeros((channels,), jnp.float32)
    high_first = jnp.zeros((channels,), jnp.float32)
    high_second = jnp.zeros((channels,), jnp.float32)
    for level_index in range(levels - 1, -1, -1):
        if level_index == shallow:
            grad_rows, carry_grad = lax.optimization_barrier((grad_rows, carry_grad))
        if level_index == shallow - 1:
            activated, carry_grad = lax.optimization_barrier((activated, carry_grad))
            act_all = lax.all_gather(activated[0], ("seq", "dp"), axis=0, tiled=True)
            weight_grad = (
                jnp.einsum(
                    "to,ti->oi",
                    grad_rows.reshape(-1, grad_rows.shape[2]),
                    act_all,
                    preferred_element_type=jnp.float32,
                )
                * grad_scale
            ).astype(jnp.bfloat16)
        spacing = 2**level_index
        current = states[level_index]
        previous = previous_list[level_index]
        weighted = level_weights[level_index] * summed_grad
        highpass = high_taps[0] * previous + high_taps[1] * current
        weight_sums[level_index] = jnp.sum(summed_grad * highpass, axis=(0, 1))
        grad_wide = carry_grad.astype(jnp.float32)
        low_first = low_first + jnp.sum(grad_wide * previous.astype(jnp.float32), axis=(0, 1))
        low_second = low_second + jnp.sum(grad_wide * current.astype(jnp.float32), axis=(0, 1))
        high_first = high_first + jnp.sum(weighted * previous.astype(jnp.float32), axis=(0, 1))
        high_second = high_second + jnp.sum(weighted * current.astype(jnp.float32), axis=(0, 1))
        carried = low_taps[0] * carry_grad + high_taps[0] * weighted
        stayed = low_taps[1] * carry_grad + high_taps[1] * weighted
        outgoing = jnp.where(
            tap_mask(positions, starts, spacing), carried, jnp.zeros_like(carried)
        ).astype(jnp.bfloat16)
        if level_index < shallow:
            border = shifted_2(outgoing[:, :spacing, :], "seq", -1)
            pulled = jnp.concatenate([outgoing[:, spacing:, :], border], axis=1)
        else:
            device_hops = spacing // row_count
            if device_hops < seq_count:
                pulled = shifted_2(outgoing, "seq", -device_hops)
            else:
                pulled = jnp.zeros_like(outgoing)
        carry_grad = (stayed + pulled).astype(jnp.bfloat16)
    token_grad = (out_grad.astype(jnp.float32) + carry_grad.astype(jnp.float32)).astype(
        jnp.bfloat16
    )
    low_grad = jnp.stack([low_first, low_second]) * grad_scale
    high_grad = jnp.stack([high_first, high_second]) * grad_scale
    level_grad = jnp.stack(weight_sums) * grad_scale
    sums = exchange_sum(jnp.concatenate([low_grad, high_grad, level_grad], axis=0), ("dp", "seq"))
    low_grad, high_grad, level_grad = sums[0:2], sums[2:4], sums[4:]
    return (result, token_grad, weight_grad, low_grad, high_grad, level_grad)


def solution(mesh):
    placed = (
        P(("groups", "dp"), "seq", "tensor"),
        P(("groups", "dp"), None),
        P(None, "tensor"),
        P(None, "tensor"),
        P(None, "tensor"),
        P(None, "tensor"),
        P(("groups", "dp"), "seq", "tensor"),
    )
    return jax.shard_map(
        shards,
        mesh=mesh,
        in_specs=placed,
        out_specs=(
            P(("groups", "dp"), "seq", "tensor"),
            P(("groups", "dp"), "seq", "tensor"),
            P(("groups", "seq", "dp"), "tensor"),
            P("groups", "tensor"),
            P("groups", "tensor"),
            P("groups", "tensor"),
        ),
        check_vma=False,
    )
```

```python
import jax
import jax.numpy as jnp
from jax import lax
from jax.sharding import PartitionSpec as P

GELU_SCALE = 0.7978845608028654
GELU_CUBIC = 0.044715


def shifted_2(block, axis, distance):
    devices = range(lax.axis_size(axis))
    route = [(i - distance, i) for i in devices if i - distance in devices]
    return lax.ppermute(block, axis, route)


def exchange_sum(values, axes):
    for axis in axes:
        size = lax.axis_size(axis)
        if size & (size - 1):
            values = lax.psum(values, axis)
            continue
        step = 1
        while step < size:
            route = [(i, i ^ step) for i in range(size)]
            values = values + lax.ppermute(values, axis, route)
            step *= 2
    return values


def exchange_scatter(values, axis):
    size = lax.axis_size(axis)
    me = lax.axis_index(axis)
    width = values.shape[-1] // size
    chunks = values.reshape(values.shape[:-1] + (size, width))

    def chunk(index):
        return lax.dynamic_index_in_dim(chunks, index, axis=chunks.ndim - 2, keepdims=False)

    total = chunk(me).astype(jnp.float32)
    for step in range(1, size):
        route = [(i, (i + step) % size) for i in range(size)]
        total = total + lax.ppermute(chunk((me + step) % size), axis, route).astype(jnp.float32)
    return total


def gelu_value(values):
    tangent = jnp.tanh(GELU_SCALE * (values + GELU_CUBIC * values * values * values))
    return 0.5 * values * (1.0 + tangent)


def gelu_slope(values):
    tangent = jnp.tanh(GELU_SCALE * (values + GELU_CUBIC * values * values * values))
    return 0.5 * (1.0 + tangent) + 0.5 * values * (1.0 - tangent * tangent) * GELU_SCALE * (
        1.0 + 3.0 * GELU_CUBIC * values * values
    )


def doc_starts(positions, doc_lengths):
    bounds = jnp.cumsum(doc_lengths, axis=1) - doc_lengths
    before = bounds[:, None, :] <= positions[None, :, None]
    return jnp.max(jnp.where(before, bounds[:, None, :], -1), axis=2)


def tap_mask(positions, starts, spacing):
    return (positions[None, :] - spacing >= starts)[:, :, None]


def shards(tokens, doc_lengths, low_taps, high_taps, level_weights, mix_weight, out_grad):
    batch_size, row_count, channels = tokens.shape
    levels = level_weights.shape[0] - 1
    seq_count = lax.axis_size("seq")
    core_count = lax.axis_size("dp")
    grad_scale = float(batch_size * row_count * seq_count * core_count) ** (-0.5)
    offset = lax.axis_index("seq") * row_count
    positions = offset + jnp.arange(row_count, dtype=jnp.int32)
    starts = doc_starts(positions, doc_lengths)
    shallow = min(levels, row_count.bit_length() - 1)
    gathered = lax.all_gather(out_grad, "tensor", axis=2, tiled=True)
    share_count = seq_count * core_count
    grad_blocks = jnp.transpose(
        gathered.reshape(row_count, share_count, gathered.shape[2] // share_count), (1, 0, 2)
    )
    grad_rows = lax.all_to_all(grad_blocks, ("seq", "dp"), 0, 0, tiled=True)
    summed = jnp.zeros(tokens.shape, jnp.float32)
    states = [tokens]
    previous_list = []
    current = tokens
    wide_positions = offset - row_count + jnp.arange(2 * row_count, dtype=jnp.int32)
    wide_starts = doc_starts(wide_positions, doc_lengths)
    wide = jnp.concatenate([shifted_2(tokens, "seq", 1), tokens], axis=1)
    for level_index in range(shallow):
        spacing = 2**level_index
        padding = jnp.zeros((wide.shape[0], spacing, wide.shape[2]), wide.dtype)
        shifted = jnp.concatenate([padding, wide[:, : 2 * row_count - spacing, :]], axis=1)
        previous_wide = jnp.where(
            tap_mask(wide_positions, wide_starts, spacing), shifted, jnp.zeros_like(shifted)
        )
        previous = previous_wide[:, row_count:, :]
        summed = summed + level_weights[level_index] * (
            high_taps[0] * previous + high_taps[1] * current
        )
        wide = (low_taps[0] * previous_wide + low_taps[1] * wide).astype(jnp.bfloat16)
        current = wide[:, row_count:, :]
        previous_list.append(previous)
        states.append(current)
    for level_index in range(shallow, levels):
        spacing = 2**level_index
        device_hops = spacing // row_count
        if device_hops < seq_count:
            shifted = shifted_2(current, "seq", device_hops)
        else:
            shifted = jnp.zeros_like(current)
        previous = jnp.where(tap_mask(positions, starts, spacing), shifted, jnp.zeros_like(shifted))
        summed = summed + level_weights[level_index] * (
            high_taps[0] * previous + high_taps[1] * current
        )
        current = (low_taps[0] * previous + low_taps[1] * current).astype(jnp.bfloat16)
        previous_list.append(previous)
        states.append(current)
    summed = summed + level_weights[levels] * current
    activated = gelu_value(summed).astype(jnp.bfloat16)
    act_grad = jnp.einsum("bro,oc->brc", gathered, mix_weight, preferred_element_type=jnp.float32)
    summed_grad = act_grad * gelu_slope(summed)
    carry_grad = (level_weights[levels] * summed_grad).astype(jnp.bfloat16)
    weight_sums = [None] * (levels + 1)
    weight_sums[levels] = jnp.sum(summed_grad * states[levels].astype(jnp.float32), axis=(0, 1))
    low_first = jnp.zeros((channels,), jnp.float32)
    low_second = jnp.zeros((channels,), jnp.float32)
    high_first = jnp.zeros((channels,), jnp.float32)
    high_second = jnp.zeros((channels,), jnp.float32)
    for level_index in range(levels - 1, -1, -1):
        if level_index == shallow:
            grad_rows, carry_grad = lax.optimization_barrier((grad_rows, carry_grad))
        if level_index == shallow:
            activated, carry_grad = lax.optimization_barrier((activated, carry_grad))
            partial_mix = jnp.einsum(
                "brc,oc->bro", activated, mix_weight, preferred_element_type=jnp.float32
            )
            mixed = exchange_scatter(partial_mix.astype(jnp.bfloat16), "tensor")
        if level_index == shallow - 1:
            activated, carry_grad = lax.optimization_barrier((activated, carry_grad))
            act_all = lax.all_gather(activated[0], ("seq", "dp"), axis=0, tiled=True)
            weight_grad = (
                jnp.einsum(
                    "to,ti->oi",
                    grad_rows.reshape(-1, grad_rows.shape[2]),
                    act_all,
                    preferred_element_type=jnp.float32,
                )
                * grad_scale
            ).astype(jnp.bfloat16)
        spacing = 2**level_index
        current = states[level_index]
        previous = previous_list[level_index]
        weighted = level_weights[level_index] * summed_grad
        highpass = high_taps[0] * previous + high_taps[1] * current
        weight_sums[level_index] = jnp.sum(summed_grad * highpass, axis=(0, 1))
        grad_wide = carry_grad.astype(jnp.float32)
        low_first = low_first + jnp.sum(grad_wide * previous.astype(jnp.float32), axis=(0, 1))
        low_second = low_second + jnp.sum(grad_wide * current.astype(jnp.float32), axis=(0, 1))
        high_first = high_first + jnp.sum(weighted * previous.astype(jnp.float32), axis=(0, 1))
        high_second = high_second + jnp.sum(weighted * current.astype(jnp.float32), axis=(0, 1))
        carried = low_taps[0] * carry_grad + high_taps[0] * weighted
        stayed = low_taps[1] * carry_grad + high_taps[1] * weighted
        outgoing = jnp.where(
            tap_mask(positions, starts, spacing), carried, jnp.zeros_like(carried)
        ).astype(jnp.bfloat16)
        if level_index < shallow:
            border = shifted_2(outgoing[:, :spacing, :], "seq", -1)
            pulled = jnp.concatenate([outgoing[:, spacing:, :], border], axis=1)
        else:
            device_hops = spacing // row_count
            if device_hops < seq_count:
                pulled = shifted_2(outgoing, "seq", -device_hops)
            else:
                pulled = jnp.zeros_like(outgoing)
        carry_grad = (stayed + pulled).astype(jnp.bfloat16)
    result = (tokens.astype(jnp.float32) + mixed).astype(jnp.bfloat16)
    token_grad = (out_grad.astype(jnp.float32) + carry_grad.astype(jnp.float32)).astype(
        jnp.bfloat16
    )
    low_grad = jnp.stack([low_first, low_second]) * grad_scale
    high_grad = jnp.stack([high_first, high_second]) * grad_scale
    level_grad = jnp.stack(weight_sums) * grad_scale
    sums = exchange_sum(jnp.concatenate([low_grad, high_grad, level_grad], axis=0), ("dp", "seq"))
    low_grad, high_grad, level_grad = sums[0:2], sums[2:4], sums[4:]
    return (result, token_grad, weight_grad, low_grad, high_grad, level_grad)


def solution(mesh):
    placed = (
        P(("groups", "dp"), "seq", "tensor"),
        P(("groups", "dp"), None),
        P(None, "tensor"),
        P(None, "tensor"),
        P(None, "tensor"),
        P(None, "tensor"),
        P(("groups", "dp"), "seq", "tensor"),
    )
    return jax.shard_map(
        shards,
        mesh=mesh,
        in_specs=placed,
        out_specs=(
            P(("groups", "dp"), "seq", "tensor"),
            P(("groups", "dp"), "seq", "tensor"),
            P(("groups", "seq", "dp"), "tensor"),
            P("groups", "tensor"),
            P("groups", "tensor"),
            P("groups", "tensor"),
        ),
        check_vma=False,
    )
```

```python
import jax
import jax.numpy as jnp
from jax import lax
from jax.sharding import PartitionSpec as P

GELU_SCALE = 0.7978845608028654
GELU_CUBIC = 0.044715


def shifted_2(block, axis, distance):
    devices = range(lax.axis_size(axis))
    route = [(i - distance, i) for i in devices if i - distance in devices]
    return lax.ppermute(block, axis, route)


def exchange_sum(values, axes):
    for axis in axes:
        size = lax.axis_size(axis)
        if size & (size - 1):
            values = lax.psum(values, axis)
            continue
        if size <= 4:
            me = lax.axis_index(axis)
            stacked = jnp.zeros((size,) + values.shape, values.dtype)
            stacked = lax.dynamic_update_index_in_dim(stacked, values, me, 0)
            for step in range(1, size):
                route = [(i, (i + step) % size) for i in range(size)]
                stacked = lax.dynamic_update_index_in_dim(
                    stacked, lax.ppermute(values, axis, route), (me - step) % size, 0
                )
            values = stacked[0]
            for index in range(1, size):
                values = values + stacked[index]
            continue
        step = 1
        while step < size:
            route = [(i, i ^ step) for i in range(size)]
            values = values + lax.ppermute(values, axis, route)
            step *= 2
    return values


def exchange_scatter(values, axis):
    size = lax.axis_size(axis)
    me = lax.axis_index(axis)
    width = values.shape[-1] // size
    chunks = values.reshape(values.shape[:-1] + (size, width))

    def chunk(index):
        return lax.dynamic_index_in_dim(chunks, index, axis=chunks.ndim - 2, keepdims=False)

    total = chunk(me).astype(jnp.float32)
    for step in range(1, size):
        route = [(i, (i + step) % size) for i in range(size)]
        total = total + lax.ppermute(chunk((me + step) % size), axis, route).astype(jnp.float32)
    return total


def gelu_value(values):
    tangent = jnp.tanh(GELU_SCALE * (values + GELU_CUBIC * values * values * values))
    return 0.5 * values * (1.0 + tangent)


def gelu_slope(values):
    tangent = jnp.tanh(GELU_SCALE * (values + GELU_CUBIC * values * values * values))
    return 0.5 * (1.0 + tangent) + 0.5 * values * (1.0 - tangent * tangent) * GELU_SCALE * (
        1.0 + 3.0 * GELU_CUBIC * values * values
    )


def doc_starts(positions, doc_lengths):
    bounds = jnp.cumsum(doc_lengths, axis=1) - doc_lengths
    before = bounds[:, None, :] <= positions[None, :, None]
    return jnp.max(jnp.where(before, bounds[:, None, :], -1), axis=2)


def tap_mask(positions, starts, spacing):
    return (positions[None, :] - spacing >= starts)[:, :, None]


def shards(tokens, doc_lengths, low_taps, high_taps, level_weights, mix_weight, out_grad):
    batch_size, row_count, channels = tokens.shape
    levels = level_weights.shape[0] - 1
    seq_count = lax.axis_size("seq")
    core_count = lax.axis_size("dp")
    grad_scale = float(batch_size * row_count * seq_count * core_count) ** (-0.5)
    offset = lax.axis_index("seq") * row_count
    positions = offset + jnp.arange(row_count, dtype=jnp.int32)
    starts = doc_starts(positions, doc_lengths)
    shallow = min(levels, row_count.bit_length() - 1)
    gathered = lax.all_gather(out_grad, "tensor", axis=2, tiled=True)
    share_count = seq_count * core_count
    grad_blocks = jnp.transpose(
        gathered.reshape(row_count, share_count, gathered.shape[2] // share_count), (1, 0, 2)
    )
    grad_rows = lax.all_to_all(grad_blocks, ("seq", "dp"), 0, 0, tiled=True)
    summed = jnp.zeros(tokens.shape, jnp.float32)
    states = [tokens]
    previous_list = []
    current = tokens
    wide_positions = offset - row_count + jnp.arange(2 * row_count, dtype=jnp.int32)
    wide_starts = doc_starts(wide_positions, doc_lengths)
    wide = jnp.concatenate([shifted_2(tokens, "seq", 1), tokens], axis=1)
    for level_index in range(shallow):
        spacing = 2**level_index
        padding = jnp.zeros((wide.shape[0], spacing, wide.shape[2]), wide.dtype)
        shifted = jnp.concatenate([padding, wide[:, : 2 * row_count - spacing, :]], axis=1)
        previous_wide = jnp.where(
            tap_mask(wide_positions, wide_starts, spacing), shifted, jnp.zeros_like(shifted)
        )
        previous = previous_wide[:, row_count:, :]
        summed = summed + level_weights[level_index] * (
            high_taps[0] * previous + high_taps[1] * current
        )
        wide = (low_taps[0] * previous_wide + low_taps[1] * wide).astype(jnp.bfloat16)
        current = wide[:, row_count:, :]
        previous_list.append(previous)
        states.append(current)
    for level_index in range(shallow, levels):
        spacing = 2**level_index
        device_hops = spacing // row_count
        if device_hops < seq_count:
            shifted = shifted_2(current, "seq", device_hops)
        else:
            shifted = jnp.zeros_like(current)
        previous = jnp.where(tap_mask(positions, starts, spacing), shifted, jnp.zeros_like(shifted))
        summed = summed + level_weights[level_index] * (
            high_taps[0] * previous + high_taps[1] * current
        )
        current = (low_taps[0] * previous + low_taps[1] * current).astype(jnp.bfloat16)
        previous_list.append(previous)
        states.append(current)
    summed = summed + level_weights[levels] * current
    activated = gelu_value(summed).astype(jnp.bfloat16)
    partial_mix = jnp.einsum(
        "brc,oc->bro", activated, mix_weight, preferred_element_type=jnp.float32
    )
    mixed = exchange_scatter(partial_mix.astype(jnp.bfloat16), "tensor")
    result = (tokens.astype(jnp.float32) + mixed).astype(jnp.bfloat16)
    act_grad = jnp.einsum("bro,oc->brc", gathered, mix_weight, preferred_element_type=jnp.float32)
    summed_grad = act_grad * gelu_slope(summed)
    carry_grad = (level_weights[levels] * summed_grad).astype(jnp.bfloat16)
    weight_sums = [None] * (levels + 1)
    weight_sums[levels] = jnp.sum(summed_grad * states[levels].astype(jnp.float32), axis=(0, 1))
    low_first = jnp.zeros((channels,), jnp.float32)
    low_second = jnp.zeros((channels,), jnp.float32)
    high_first = jnp.zeros((channels,), jnp.float32)
    high_second = jnp.zeros((channels,), jnp.float32)
    for level_index in range(levels - 1, -1, -1):
        if level_index == shallow:
            grad_rows, carry_grad = lax.optimization_barrier((grad_rows, carry_grad))
        if level_index == shallow - 1:
            activated, carry_grad = lax.optimization_barrier((activated, carry_grad))
            act_all = lax.all_gather(activated[0], ("seq", "dp"), axis=0, tiled=True)
            weight_grad = (
                jnp.einsum(
                    "to,ti->oi",
                    grad_rows.reshape(-1, grad_rows.shape[2]),
                    act_all,
                    preferred_element_type=jnp.float32,
                )
                * grad_scale
            ).astype(jnp.bfloat16)
        spacing = 2**level_index
        current = states[level_index]
        previous = previous_list[level_index]
        weighted = level_weights[level_index] * summed_grad
        highpass = high_taps[0] * previous + high_taps[1] * current
        weight_sums[level_index] = jnp.sum(summed_grad * highpass, axis=(0, 1))
        grad_wide = carry_grad.astype(jnp.float32)
        low_first = low_first + jnp.sum(grad_wide * previous.astype(jnp.float32), axis=(0, 1))
        low_second = low_second + jnp.sum(grad_wide * current.astype(jnp.float32), axis=(0, 1))
        high_first = high_first + jnp.sum(weighted * previous.astype(jnp.float32), axis=(0, 1))
        high_second = high_second + jnp.sum(weighted * current.astype(jnp.float32), axis=(0, 1))
        carried = low_taps[0] * carry_grad + high_taps[0] * weighted
        stayed = low_taps[1] * carry_grad + high_taps[1] * weighted
        outgoing = jnp.where(
            tap_mask(positions, starts, spacing), carried, jnp.zeros_like(carried)
        ).astype(jnp.bfloat16)
        if level_index < shallow:
            border = shifted_2(outgoing[:, :spacing, :], "seq", -1)
            pulled = jnp.concatenate([outgoing[:, spacing:, :], border], axis=1)
        else:
            device_hops = spacing // row_count
            if device_hops < seq_count:
                pulled = shifted_2(outgoing, "seq", -device_hops)
            else:
                pulled = jnp.zeros_like(outgoing)
        carry_grad = (stayed + pulled).astype(jnp.bfloat16)
    token_grad = (out_grad.astype(jnp.float32) + carry_grad.astype(jnp.float32)).astype(
        jnp.bfloat16
    )
    low_grad = jnp.stack([low_first, low_second]) * grad_scale
    high_grad = jnp.stack([high_first, high_second]) * grad_scale
    level_grad = jnp.stack(weight_sums) * grad_scale
    sums = exchange_sum(jnp.concatenate([low_grad, high_grad, level_grad], axis=0), ("dp", "seq"))
    low_grad, high_grad, level_grad = sums[0:2], sums[2:4], sums[4:]
    return (result, token_grad, weight_grad, low_grad, high_grad, level_grad)


def solution(mesh):
    placed = (
        P(("groups", "dp"), "seq", "tensor"),
        P(("groups", "dp"), None),
        P(None, "tensor"),
        P(None, "tensor"),
        P(None, "tensor"),
        P(None, "tensor"),
        P(("groups", "dp"), "seq", "tensor"),
    )
    return jax.shard_map(
        shards,
        mesh=mesh,
        in_specs=placed,
        out_specs=(
            P(("groups", "dp"), "seq", "tensor"),
            P(("groups", "dp"), "seq", "tensor"),
            P(("groups", "seq", "dp"), "tensor"),
            P("groups", "tensor"),
            P("groups", "tensor"),
            P("groups", "tensor"),
        ),
        check_vma=False,
    )
```

```python
import jax
import jax.numpy as jnp
from jax import lax
from jax.sharding import PartitionSpec as P

GELU_SCALE = 0.7978845608028654
GELU_CUBIC = 0.044715


def shifted_2(block, axis, distance):
    devices = range(lax.axis_size(axis))
    route = [(i - distance, i) for i in devices if i - distance in devices]
    return lax.ppermute(block, axis, route)


def exchange_sum(values, axes):
    for axis in axes:
        size = lax.axis_size(axis)
        if size & (size - 1):
            values = lax.psum(values, axis)
            continue
        if size <= 4:
            me = lax.axis_index(axis)
            stacked = jnp.zeros((size,) + values.shape, values.dtype)
            stacked = lax.dynamic_update_index_in_dim(stacked, values, me, 0)
            for step in range(1, size):
                route = [(i, (i + step) % size) for i in range(size)]
                stacked = lax.dynamic_update_index_in_dim(
                    stacked, lax.ppermute(values, axis, route), (me - step) % size, 0
                )
            values = stacked[0]
            for index in range(1, size):
                values = values + stacked[index]
            continue
        step = 1
        while step < size:
            route = [(i, i ^ step) for i in range(size)]
            values = values + lax.ppermute(values, axis, route)
            step *= 2
    return values


def exchange_scatter(values, axis):
    size = lax.axis_size(axis)
    me = lax.axis_index(axis)
    width = values.shape[-1] // size
    chunks = values.reshape(values.shape[:-1] + (size, width))

    def chunk(index):
        return lax.dynamic_index_in_dim(chunks, index, axis=chunks.ndim - 2, keepdims=False)

    total = chunk(me).astype(jnp.float32)
    for step in range(1, size):
        route = [(i, (i + step) % size) for i in range(size)]
        total = total + lax.ppermute(chunk((me + step) % size), axis, route).astype(jnp.float32)
    return total


def gelu_value(values):
    tangent = jnp.tanh(GELU_SCALE * (values + GELU_CUBIC * values * values * values))
    return 0.5 * values * (1.0 + tangent)


def gelu_slope(values):
    tangent = jnp.tanh(GELU_SCALE * (values + GELU_CUBIC * values * values * values))
    return 0.5 * (1.0 + tangent) + 0.5 * values * (1.0 - tangent * tangent) * GELU_SCALE * (
        1.0 + 3.0 * GELU_CUBIC * values * values
    )


def doc_starts(positions, doc_lengths):
    bounds = jnp.cumsum(doc_lengths, axis=1) - doc_lengths
    before = bounds[:, None, :] <= positions[None, :, None]
    return jnp.max(jnp.where(before, bounds[:, None, :], -1), axis=2)


def tap_mask(positions, starts, spacing):
    return (positions[None, :] - spacing >= starts)[:, :, None]


def shards(tokens, doc_lengths, low_taps, high_taps, level_weights, mix_weight, out_grad):
    batch_size, row_count, channels = tokens.shape
    levels = level_weights.shape[0] - 1
    seq_count = lax.axis_size("seq")
    core_count = lax.axis_size("dp")
    grad_scale = float(batch_size * row_count * seq_count * core_count) ** (-0.5)
    offset = lax.axis_index("seq") * row_count
    positions = offset + jnp.arange(row_count, dtype=jnp.int32)
    starts = doc_starts(positions, doc_lengths)
    shallow = min(levels, row_count.bit_length() - 1)
    gathered = lax.all_gather(out_grad, "tensor", axis=2, tiled=True)
    share_count = seq_count * core_count
    grad_blocks = jnp.transpose(
        gathered.reshape(row_count, share_count, gathered.shape[2] // share_count), (1, 0, 2)
    )
    grad_rows = lax.all_to_all(grad_blocks, ("seq", "dp"), 0, 0, tiled=True)
    summed = jnp.zeros(tokens.shape, jnp.float32)
    states = [tokens]
    previous_list = []
    current = tokens
    wide_positions = offset - row_count + jnp.arange(2 * row_count, dtype=jnp.int32)
    wide_starts = doc_starts(wide_positions, doc_lengths)
    wide = jnp.concatenate([shifted_2(tokens, "seq", 1), tokens], axis=1)
    for level_index in range(shallow):
        spacing = 2**level_index
        padding = jnp.zeros((wide.shape[0], spacing, wide.shape[2]), wide.dtype)
        shifted = jnp.concatenate([padding, wide[:, : 2 * row_count - spacing, :]], axis=1)
        previous_wide = jnp.where(
            tap_mask(wide_positions, wide_starts, spacing), shifted, jnp.zeros_like(shifted)
        )
        previous = previous_wide[:, row_count:, :]
        summed = summed + level_weights[level_index] * (
            high_taps[0] * previous + high_taps[1] * current
        )
        wide = (low_taps[0] * previous_wide + low_taps[1] * wide).astype(jnp.bfloat16)
        current = wide[:, row_count:, :]
        previous_list.append(previous)
        states.append(current)
    for level_index in range(shallow, levels):
        spacing = 2**level_index
        device_hops = spacing // row_count
        if device_hops < seq_count:
            shifted = shifted_2(current, "seq", device_hops)
        else:
            shifted = jnp.zeros_like(current)
        previous = jnp.where(tap_mask(positions, starts, spacing), shifted, jnp.zeros_like(shifted))
        summed = summed + level_weights[level_index] * (
            high_taps[0] * previous + high_taps[1] * current
        )
        current = (low_taps[0] * previous + low_taps[1] * current).astype(jnp.bfloat16)
        previous_list.append(previous)
        states.append(current)
    summed = summed + level_weights[levels] * current
    activated = gelu_value(summed).astype(jnp.bfloat16)
    partial_mix = jnp.einsum(
        "brc,oc->bro", activated, mix_weight, preferred_element_type=jnp.float32
    )
    mixed = exchange_scatter(partial_mix.astype(jnp.bfloat16), "tensor")
    result = (tokens.astype(jnp.float32) + mixed).astype(jnp.bfloat16)
    act_grad = jnp.einsum("bro,oc->brc", gathered, mix_weight, preferred_element_type=jnp.float32)
    summed_grad = act_grad * gelu_slope(summed)
    carry_grad = (level_weights[levels] * summed_grad).astype(jnp.bfloat16)
    weight_sums = [None] * (levels + 1)
    weight_sums[levels] = jnp.sum(summed_grad * states[levels].astype(jnp.float32), axis=(0, 1))
    low_first = jnp.zeros((channels,), jnp.float32)
    low_second = jnp.zeros((channels,), jnp.float32)
    high_first = jnp.zeros((channels,), jnp.float32)
    high_second = jnp.zeros((channels,), jnp.float32)
    for level_index in range(levels - 1, -1, -1):
        if level_index == shallow:
            grad_rows, carry_grad = lax.optimization_barrier((grad_rows, carry_grad))
        if level_index == shallow:
            activated, carry_grad = lax.optimization_barrier((activated, carry_grad))
            act_all = lax.all_gather(activated[0], ("seq", "dp"), axis=0, tiled=True)
            weight_grad = (
                jnp.einsum(
                    "to,ti->oi",
                    grad_rows.reshape(-1, grad_rows.shape[2]),
                    act_all,
                    preferred_element_type=jnp.float32,
                )
                * grad_scale
            ).astype(jnp.bfloat16)
        spacing = 2**level_index
        current = states[level_index]
        previous = previous_list[level_index]
        weighted = level_weights[level_index] * summed_grad
        highpass = high_taps[0] * previous + high_taps[1] * current
        weight_sums[level_index] = jnp.sum(summed_grad * highpass, axis=(0, 1))
        grad_wide = carry_grad.astype(jnp.float32)
        low_first = low_first + jnp.sum(grad_wide * previous.astype(jnp.float32), axis=(0, 1))
        low_second = low_second + jnp.sum(grad_wide * current.astype(jnp.float32), axis=(0, 1))
        high_first = high_first + jnp.sum(weighted * previous.astype(jnp.float32), axis=(0, 1))
        high_second = high_second + jnp.sum(weighted * current.astype(jnp.float32), axis=(0, 1))
        carried = low_taps[0] * carry_grad + high_taps[0] * weighted
        stayed = low_taps[1] * carry_grad + high_taps[1] * weighted
        outgoing = jnp.where(
            tap_mask(positions, starts, spacing), carried, jnp.zeros_like(carried)
        ).astype(jnp.bfloat16)
        if level_index < shallow:
            border = shifted_2(outgoing[:, :spacing, :], "seq", -1)
            pulled = jnp.concatenate([outgoing[:, spacing:, :], border], axis=1)
        else:
            device_hops = spacing // row_count
            if device_hops < seq_count:
                pulled = shifted_2(outgoing, "seq", -device_hops)
            else:
                pulled = jnp.zeros_like(outgoing)
        carry_grad = (stayed + pulled).astype(jnp.bfloat16)
    token_grad = (out_grad.astype(jnp.float32) + carry_grad.astype(jnp.float32)).astype(
        jnp.bfloat16
    )
    low_grad = jnp.stack([low_first, low_second]) * grad_scale
    high_grad = jnp.stack([high_first, high_second]) * grad_scale
    level_grad = jnp.stack(weight_sums) * grad_scale
    sums = exchange_sum(jnp.concatenate([low_grad, high_grad, level_grad], axis=0), ("dp", "seq"))
    low_grad, high_grad, level_grad = sums[0:2], sums[2:4], sums[4:]
    return (result, token_grad, weight_grad, low_grad, high_grad, level_grad)


def solution(mesh):
    placed = (
        P(("groups", "dp"), "seq", "tensor"),
        P(("groups", "dp"), None),
        P(None, "tensor"),
        P(None, "tensor"),
        P(None, "tensor"),
        P(None, "tensor"),
        P(("groups", "dp"), "seq", "tensor"),
    )
    return jax.shard_map(
        shards,
        mesh=mesh,
        in_specs=placed,
        out_specs=(
            P(("groups", "dp"), "seq", "tensor"),
            P(("groups", "dp"), "seq", "tensor"),
            P(("groups", "seq", "dp"), "tensor"),
            P("groups", "tensor"),
            P("groups", "tensor"),
            P("groups", "tensor"),
        ),
        check_vma=False,
    )
```

```python
import jax
import jax.numpy as jnp
from jax import lax
from jax.sharding import PartitionSpec as P

GELU_SCALE = 0.7978845608028654
GELU_CUBIC = 0.044715


def shifted_2(block, axis, distance):
    devices = range(lax.axis_size(axis))
    route = [(i - distance, i) for i in devices if i - distance in devices]
    return lax.ppermute(block, axis, route)


def exchange_sum(values, axes):
    for axis in axes:
        size = lax.axis_size(axis)
        if size & (size - 1):
            values = lax.psum(values, axis)
            continue
        if size <= 4:
            me = lax.axis_index(axis)
            stacked = jnp.zeros((size,) + values.shape, values.dtype)
            stacked = lax.dynamic_update_index_in_dim(stacked, values, me, 0)
            for step in range(1, size):
                route = [(i, (i + step) % size) for i in range(size)]
                stacked = lax.dynamic_update_index_in_dim(
                    stacked, lax.ppermute(values, axis, route), (me - step) % size, 0
                )
            values = stacked[0]
            for index in range(1, size):
                values = values + stacked[index]
            continue
        step = 1
        while step < size:
            route = [(i, i ^ step) for i in range(size)]
            values = values + lax.ppermute(values, axis, route)
            step *= 2
    return values


def exchange_scatter(values, axis):
    size = lax.axis_size(axis)
    me = lax.axis_index(axis)
    width = values.shape[-1] // size
    chunks = values.reshape(values.shape[:-1] + (size, width))

    def chunk(index):
        return lax.dynamic_index_in_dim(chunks, index, axis=chunks.ndim - 2, keepdims=False)

    total = chunk(me).astype(jnp.float32)
    for step in range(1, size):
        route = [(i, (i + step) % size) for i in range(size)]
        total = total + lax.ppermute(chunk((me + step) % size), axis, route).astype(jnp.float32)
    return total


def gelu_value(values):
    tangent = jnp.tanh(GELU_SCALE * (values + GELU_CUBIC * values * values * values))
    return 0.5 * values * (1.0 + tangent)


def gelu_slope(values):
    tangent = jnp.tanh(GELU_SCALE * (values + GELU_CUBIC * values * values * values))
    return 0.5 * (1.0 + tangent) + 0.5 * values * (1.0 - tangent * tangent) * GELU_SCALE * (
        1.0 + 3.0 * GELU_CUBIC * values * values
    )


def doc_starts(positions, doc_lengths):
    bounds = jnp.cumsum(doc_lengths, axis=1) - doc_lengths
    before = bounds[:, None, :] <= positions[None, :, None]
    return jnp.max(jnp.where(before, bounds[:, None, :], -1), axis=2)


def tap_mask(positions, starts, spacing):
    return (positions[None, :] - spacing >= starts)[:, :, None]


def shards(tokens, doc_lengths, low_taps, high_taps, level_weights, mix_weight, out_grad):
    batch_size, row_count, channels = tokens.shape
    levels = level_weights.shape[0] - 1
    seq_count = lax.axis_size("seq")
    core_count = lax.axis_size("dp")
    grad_scale = float(batch_size * row_count * seq_count * core_count) ** (-0.5)
    offset = lax.axis_index("seq") * row_count
    positions = offset + jnp.arange(row_count, dtype=jnp.int32)
    starts = doc_starts(positions, doc_lengths)
    shallow = min(levels, row_count.bit_length() - 1)
    gathered = lax.all_gather(out_grad, "tensor", axis=2, tiled=True)
    share_count = seq_count * core_count
    grad_blocks = jnp.transpose(
        gathered.reshape(row_count, share_count, gathered.shape[2] // share_count), (1, 0, 2)
    )
    grad_rows = lax.all_to_all(grad_blocks, ("seq", "dp"), 0, 0, tiled=True)
    summed = jnp.zeros(tokens.shape, jnp.float32)
    states = [tokens]
    previous_list = []
    current = tokens
    wide_positions = offset - row_count + jnp.arange(2 * row_count, dtype=jnp.int32)
    wide_starts = doc_starts(wide_positions, doc_lengths)
    wide = jnp.concatenate([shifted_2(tokens, "seq", 1), tokens], axis=1)
    for level_index in range(shallow):
        spacing = 2**level_index
        padding = jnp.zeros((wide.shape[0], spacing, wide.shape[2]), wide.dtype)
        shifted = jnp.concatenate([padding, wide[:, : 2 * row_count - spacing, :]], axis=1)
        previous_wide = jnp.where(
            tap_mask(wide_positions, wide_starts, spacing), shifted, jnp.zeros_like(shifted)
        )
        previous = previous_wide[:, row_count:, :]
        summed = summed + level_weights[level_index] * (
            high_taps[0] * previous + high_taps[1] * current
        )
        wide = (low_taps[0] * previous_wide + low_taps[1] * wide).astype(jnp.bfloat16)
        current = wide[:, row_count:, :]
        previous_list.append(previous)
        states.append(current)
    for level_index in range(shallow, levels):
        spacing = 2**level_index
        device_hops = spacing // row_count
        if device_hops < seq_count:
            shifted = shifted_2(current, "seq", device_hops)
        else:
            shifted = jnp.zeros_like(current)
        previous = jnp.where(tap_mask(positions, starts, spacing), shifted, jnp.zeros_like(shifted))
        summed = summed + level_weights[level_index] * (
            high_taps[0] * previous + high_taps[1] * current
        )
        current = (low_taps[0] * previous + low_taps[1] * current).astype(jnp.bfloat16)
        previous_list.append(previous)
        states.append(current)
    summed = summed + level_weights[levels] * current
    activated = gelu_value(summed).astype(jnp.bfloat16)
    partial_mix = jnp.einsum(
        "brc,oc->bro", activated, mix_weight, preferred_element_type=jnp.float32
    )
    mixed = exchange_scatter(partial_mix.astype(jnp.bfloat16), "tensor")
    result = (tokens.astype(jnp.float32) + mixed).astype(jnp.bfloat16)
    act_grad = jnp.einsum("bro,oc->brc", gathered, mix_weight, preferred_element_type=jnp.float32)
    summed_grad = act_grad * gelu_slope(summed)
    carry_grad = (level_weights[levels] * summed_grad).astype(jnp.bfloat16)
    weight_sums = [None] * (levels + 1)
    weight_sums[levels] = jnp.sum(summed_grad * states[levels].astype(jnp.float32), axis=(0, 1))
    low_first = jnp.zeros((channels,), jnp.float32)
    low_second = jnp.zeros((channels,), jnp.float32)
    high_first = jnp.zeros((channels,), jnp.float32)
    high_second = jnp.zeros((channels,), jnp.float32)
    for level_index in range(levels - 1, -1, -1):
        if level_index == shallow:
            grad_rows, carry_grad = lax.optimization_barrier((grad_rows, carry_grad))
        if level_index == min(shallow + 1, levels - 1):
            activated, carry_grad = lax.optimization_barrier((activated, carry_grad))
            act_all = lax.all_gather(activated[0], ("seq", "dp"), axis=0, tiled=True)
            weight_grad = (
                jnp.einsum(
                    "to,ti->oi",
                    grad_rows.reshape(-1, grad_rows.shape[2]),
                    act_all,
                    preferred_element_type=jnp.float32,
                )
                * grad_scale
            ).astype(jnp.bfloat16)
        spacing = 2**level_index
        current = states[level_index]
        previous = previous_list[level_index]
        weighted = level_weights[level_index] * summed_grad
        highpass = high_taps[0] * previous + high_taps[1] * current
        weight_sums[level_index] = jnp.sum(summed_grad * highpass, axis=(0, 1))
        grad_wide = carry_grad.astype(jnp.float32)
        low_first = low_first + jnp.sum(grad_wide * previous.astype(jnp.float32), axis=(0, 1))
        low_second = low_second + jnp.sum(grad_wide * current.astype(jnp.float32), axis=(0, 1))
        high_first = high_first + jnp.sum(weighted * previous.astype(jnp.float32), axis=(0, 1))
        high_second = high_second + jnp.sum(weighted * current.astype(jnp.float32), axis=(0, 1))
        carried = low_taps[0] * carry_grad + high_taps[0] * weighted
        stayed = low_taps[1] * carry_grad + high_taps[1] * weighted
        outgoing = jnp.where(
            tap_mask(positions, starts, spacing), carried, jnp.zeros_like(carried)
        ).astype(jnp.bfloat16)
        if level_index < shallow:
            border = shifted_2(outgoing[:, :spacing, :], "seq", -1)
            pulled = jnp.concatenate([outgoing[:, spacing:, :], border], axis=1)
        else:
            device_hops = spacing // row_count
            if device_hops < seq_count:
                pulled = shifted_2(outgoing, "seq", -device_hops)
            else:
                pulled = jnp.zeros_like(outgoing)
        carry_grad = (stayed + pulled).astype(jnp.bfloat16)
    token_grad = (out_grad.astype(jnp.float32) + carry_grad.astype(jnp.float32)).astype(
        jnp.bfloat16
    )
    low_grad = jnp.stack([low_first, low_second]) * grad_scale
    high_grad = jnp.stack([high_first, high_second]) * grad_scale
    level_grad = jnp.stack(weight_sums) * grad_scale
    sums = exchange_sum(jnp.concatenate([low_grad, high_grad, level_grad], axis=0), ("dp", "seq"))
    low_grad, high_grad, level_grad = sums[0:2], sums[2:4], sums[4:]
    return (result, token_grad, weight_grad, low_grad, high_grad, level_grad)


def solution(mesh):
    placed = (
        P(("groups", "dp"), "seq", "tensor"),
        P(("groups", "dp"), None),
        P(None, "tensor"),
        P(None, "tensor"),
        P(None, "tensor"),
        P(None, "tensor"),
        P(("groups", "dp"), "seq", "tensor"),
    )
    return jax.shard_map(
        shards,
        mesh=mesh,
        in_specs=placed,
        out_specs=(
            P(("groups", "dp"), "seq", "tensor"),
            P(("groups", "dp"), "seq", "tensor"),
            P(("groups", "seq", "dp"), "tensor"),
            P("groups", "tensor"),
            P("groups", "tensor"),
            P("groups", "tensor"),
        ),
        check_vma=False,
    )
```
